128 devices in a mesh: req: 8 (over y, core), exp: 16 (over z, x).
Axes of the slice: x: 4, y: 4, z: 4, core: 2. Of those that a mesh axis runs over, the one named last changes fastest.
Arguments:
- queries: bfloat16 [128, 64, 2048], P('req', None, 'exp'), may hold values from -42 to 42
- new_keys: bfloat16 [128, 64, 2048], P('req', None, 'exp'), may hold values from -6 to 6
- new_values: bfloat16 [128, 64, 2048], P('req', None, 'exp'), may hold values from -6 to 6
- long_keys: bfloat16 [8, 16384, 2048], P('req', None, 'exp'), may hold values from -18 to 18
- long_values: bfloat16 [8, 16384, 2048], P('req', None, 'exp'), may hold values from -6 to 6
- long_lengths: int32 [8], P('req'), may hold values from 4096 to 16384
- short_keys: bfloat16 [120, 1024, 2048], P('req', None, 'exp'), may hold values from -18 to 18
- short_values: bfloat16 [120, 1024, 2048], P('req', None, 'exp'), may hold values from -6 to 6
- short_lengths: int32 [120], P('req'), may hold values from 256 to 1024
- parents: int32 [128, 64], P('req'), may hold values from 0 to 62, as said below
- accepted: int32 [128], P('req'), may hold values from 0 to 63
- residual: float32 [8192, 2048], P(('req', 'exp')), may hold values from -18 to 18
- out_weight: bfloat16 [2048, 2048], P('exp'), may hold values from -2 to 2
- norm_gain: float32 [2048], replicated, may hold values from 0.5 to 1.5
- routes: int32 [8192, 8], P(('req', 'exp')), may hold values from 0 to 63, all different within a row; in each aligned block of 64 rows (0 to 63, 64 to 127, ...) at most 16 rows name the same one
- route_weights: float32 [8192, 8], P(('req', 'exp')), may hold values from 0.05 to 0.4
- expert_gate: bfloat16 [128, 2048, 512], P(('req', 'exp')), may hold values from -0.125 to 0.125
- expert_up: bfloat16 [128, 2048, 512], P(('req', 'exp')), may hold values from -0.125 to 0.125
- expert_down: bfloat16 [128, 512, 2048], P(('req', 'exp')), may hold values from -0.1875 to 0.1875
Outputs:
- hidden_out: bfloat16 [8192, 2048], P(('req', 'exp'))
- accepted_keys: bfloat16 [128, 64, 2048], P('req', None, 'exp')
- accepted_values: bfloat16 [128, 64, 2048], P('req', None, 'exp')
The draws below stay inside these ranges and needn't reach their ends.
Inputs may be any that keep to these rules, and one draw needn't show every extreme that they name: parents[r, 0] = 0 (the root); for t >= 1, parents[r, t] < t. `routes`: each row names 8 different experts; within the 64 rows of one device (aligned blocks) no expert is named by more than 16 rows.
All inputs are finite; a program needn't handle non-finite values.
Results may differ from the reference program's by a relative error of at most 0.02.
Values may be sent and summed in bfloat16 or wider, within the bound.
No kernel may reach another device: no remote copies, remote signals or barrier semaphores. Data moves between devices by JAX's collectives and lax.ppermute only.
A program may use at most 128 MiB of HBM per device.

```python
import math
import jax
import jax.numpy as jnp
import numpy as np
from jax import lax

D = 2048
HEAD = 128
FF = 1024
EXPERTS = 64
TOPK = 8
DRAFT = 64
LMAX = 16384
SMAX = 1024
SHORT_DEV = 15
HD = 2048
REQ_DEV = 16
LONG = 8
SHORT = 120
REQS = 128
TOKENS = 8192
TOK_DEV = 64
PIECES = 2
FF_DEV = 512
SLICES = 128
CAP = 16
N_REQ = 8
N_EXP = 16


def first_rows(key, number):
    return jax.random.truncated_normal(jax.random.fold_in(key, 1), -6.0, 6.0, (number, 1, HD), jnp.float32)


def cache_rows(key, number, positions):
    first = first_rows(key, number)
    others = jax.random.truncated_normal(jax.random.fold_in(key, 2), -6.0, 6.0, (number, positions - 1, HD), jnp.float32)
    return jnp.concatenate([first, others], axis=1)


def draw_long_keys(key, part):
    return cache_rows(jax.random.fold_in(key, 101), LONG, LMAX).astype(jnp.bfloat16)


def draw_short_keys(key, part):
    return cache_rows(jax.random.fold_in(key, 102), SHORT, SMAX).astype(jnp.bfloat16)


def draw_queries(key, part):
    base = jax.random.truncated_normal(jax.random.fold_in(key, 103), -6.0, 6.0, (REQS, DRAFT, HD), jnp.float32)
    return base.astype(jnp.bfloat16)


def draw_long_lengths(key, part):
    drawn = jax.random.randint(jax.random.fold_in(key, 104), (LONG,), LMAX // 4, LMAX + 1, dtype=jnp.int32)
    return jnp.where(jnp.arange(LONG, dtype=jnp.int32) == 0, LMAX, drawn).astype(jnp.int32)


def draw_short_lengths(key, part):
    drawn = jax.random.randint(jax.random.fold_in(key, 105), (SHORT,), SMAX // 4, SMAX + 1, dtype=jnp.int32)
    return jnp.where(jnp.arange(SHORT, dtype=jnp.int32) == 0, SMAX, drawn).astype(jnp.int32)


def draw_parents(key, part):
    position = jnp.arange(DRAFT, dtype=jnp.int32)
    upper = jnp.broadcast_to(jnp.maximum(position, 1)[None, :], (REQS, DRAFT))
    drawn = jax.random.randint(jax.random.fold_in(key, 106), (REQS, DRAFT), 0, upper, dtype=jnp.int32)
    request = jnp.arange(REQS, dtype=jnp.int32)
    pinned = (request[:, None] == 0) & (position[None, :] == DRAFT - 1)
    return jnp.where(pinned, DRAFT - 2, drawn).astype(jnp.int32)


def draw_residual(key, part):
    row_scale = jnp.exp(jax.random.uniform(jax.random.fold_in(key, 107), (TOKENS, 1), jnp.float32, math.log(0.1), 0.0))
    col_scale = jnp.exp(jax.random.uniform(jax.random.fold_in(key, 108), (1, D), jnp.float32, math.log(0.3), math.log(3.0)))
    noise = jax.random.truncated_normal(jax.random.fold_in(key, 110), -6.0, 6.0, (TOKENS, D), jnp.float32)
    return noise * row_scale * col_scale


def touch_ends(values, own_key, low, high):
    extent = values.shape
    place = [jax.random.randint(jax.random.fold_in(own_key, axis), (), 0, extent[axis]) for axis in range(len(extent))]
    values = values.at[tuple(place)].set(low)
    longest = extent.index(max(extent))
    place[longest] = (place[longest] + 1) % extent[longest]
    return values.at[tuple(place)].set(high)


def level_of(own_key, dims, split, smallest, high):
    gain, own = 1.0, jax.random.fold_in(own_key, 6)
    for dim, parts in split:
        heights = jnp.exp(jax.random.uniform(jax.random.fold_in(own, dim), (parts,), jnp.float32, smallest / len(split), high / len(split)))
        gain = gain * jnp.repeat(heights, dims[dim] // parts).reshape([-1 if axis == dim else 1 for axis in range(len(dims))])
    return gain


def routed_block(key, own, number, rows, amount, top, limit, slope):
    ranking = jax.random.permutation(key, amount)
    crowded, usual = shares(amount, rows * top, limit, slope, True), shares(amount, rows * top, limit, slope, False)
    places = jnp.arange(amount)

    def named(sizes, offset_by):
        used = int((sizes > 0).sum())
        fixed = max(1, used // 4)
        moved = fixed + (places - fixed + offset_by * (used - fixed)) % max(1, amount - fixed)
        return jnp.zeros((amount,), jnp.int32).at[ranking[jnp.where(places < fixed, places, moved)]].set(jnp.asarray(sizes, jnp.int32))

    sizes = jnp.where(number % 4 == 0, named(crowded, number // 4), named(usual, number - number // 4 - 1))
    mixed = jax.random.permutation(jax.random.fold_in(own, 3), amount)
    donor, taker = mixed[0:amount // 2 * 2:2], mixed[1:amount // 2 * 2:2]
    slack = jnp.minimum(sizes[donor] - 1, limit - sizes[taker]) // 2
    slack = jnp.where((donor == ranking[0]) | (taker == ranking[0]) | (sizes[taker] == 0), 0, jnp.maximum(slack, 0))
    moved = jax.random.randint(jax.random.fold_in(own, 4), (amount // 2,), 0, 1 << 20) % (slack + 1)
    sizes = sizes.at[donor].add(-moved).at[taker].add(moved)
    labels = jnp.searchsorted(jnp.cumsum(sizes), jnp.arange(rows * top), side="right").astype(jnp.int32)
    grid = labels.reshape(top, rows).T
    grid = grid[jax.random.permutation(jax.random.fold_in(own, 1), rows)]
    offset_by = jax.random.randint(jax.random.fold_in(own, 2), (rows, 1), 0, top)
    return jnp.take_along_axis(grid, (jnp.arange(top)[None, :] + offset_by) % top, axis=1)


def shares(count, total, reach, lean, full):
    weights = [(1 << 20) // math.isqrt(standing ** lean) + 1 for standing in range(1, count + 1)]
    largest = reach if full else min(reach, max(-(-total // count), total * weights[0] // sum(weights)))
    least = 1 if total - largest >= count - 1 else 0
    counts, rest = [largest] + [least] * (count - 1), total - largest - least * (count - 1)
    while rest > 0:
        movable = [i for i in range(1, count) if counts[i] < largest] or [i for i in range(1, count) if counts[i] < reach]
        whole, budget = sum([weights[i] for i in movable]), rest
        for i in movable:
            more = min(reach - counts[i], max(1, budget * weights[i] // whole), rest)
            counts[i] = counts[i] + more
            rest = rest - more
    return np.array(counts)


def normal_values(own_key, extent, deviation, most, cuts=(), kind=jnp.bfloat16):
    values = jax.random.normal(own_key, extent, jnp.float32) * deviation
    if len(cuts) > 0:
        values = level_of(own_key, extent, cuts, -0.22, 0.18) * values
    return jnp.clip(values, min=-most, max=most).astype(kind)


def setup_inputs(seed: int = 0) -> dict:
    key_of = jax.random.split(jax.random.key(seed), 20)
    queries = draw_queries(jax.random.fold_in(key_of[19], 71), 0)
    new_keys = normal_values(key_of[1], (REQS, DRAFT, HD), 1.0, 6.0, ((0, 8), (2, 16)))
    new_values = normal_values(key_of[2], (REQS, DRAFT, HD), 1.0, 6.0, ((0, 8), (2, 16)))
    long_keys = draw_long_keys(jax.random.fold_in(key_of[19], 71), 0)
    long_values = normal_values(key_of[4], (LONG, LMAX, HD), 1.0, 6.0, ((0, 8), (2, 16)))
    long_lengths = draw_long_lengths(jax.random.fold_in(key_of[19], 71), 0)
    short_keys = draw_short_keys(jax.random.fold_in(key_of[19], 71), 0)
    short_values = normal_values(key_of[7], (SHORT, SMAX, HD), 1.0, 6.0, ((0, 8), (2, 16)))
    short_lengths = draw_short_lengths(jax.random.fold_in(key_of[19], 71), 0)
    parents = draw_parents(jax.random.fold_in(key_of[19], 71), 0)
    accepted = touch_ends(jax.random.randint(key_of[10], (REQS,), 0, DRAFT), jax.random.fold_in(key_of[10], 1), 0, DRAFT - 1).astype(jnp.int32)
    residual = draw_residual(jax.random.fold_in(key_of[19], 71), 0)
    out_weight = normal_values(key_of[12], (HD, D), 8 ** -0.5, 2.0, ((0, 16),))
    norm_gain = jnp.clip(1.0 + 0.1 * jax.random.normal(key_of[13], (D,), jnp.float32), 0.5, 1.5)
    routes_keys = jax.random.split(jax.random.fold_in(key_of[14], 1), TOKENS // TOK_DEV)
    routes_turns = jax.random.permutation(jax.random.fold_in(key_of[14], 3), TOKENS // TOK_DEV)
    routes = jax.vmap(lambda own, number: routed_block(jax.random.fold_in(key_of[14], 2), own, number, TOK_DEV, EXPERTS, TOPK, CAP, 2))(routes_keys, routes_turns).reshape((TOKENS, TOPK))
    route_weights = jnp.clip(0.05 + 0.35 * jax.random.uniform(key_of[15], (TOKENS, TOPK), jnp.float32) ** level_of(key_of[15], (TOKENS, TOPK), ((0, 128),), -0.2, 0.2), 0.05, 0.4)
    expert_gate = normal_values(key_of[16], (SLICES, D, FF_DEV), D ** -0.5, 0.125, ((0, 128),))
    expert_up = normal_values(key_of[17], (SLICES, D, FF_DEV), D ** -0.5, 0.125, ((0, 128),))
    expert_down = normal_values(key_of[18], (SLICES, FF_DEV, D), FF ** -0.5, 0.1875, ((0, 128),))
    return {"queries": queries, "new_keys": new_keys, "new_values": new_values, "long_keys": long_keys, "long_values": long_values, "long_lengths": long_lengths, "short_keys": short_keys, "short_values": short_values, "short_lengths": short_lengths, "parents": parents, "accepted": accepted, "residual": residual, "out_weight": out_weight, "norm_gain": norm_gain, "routes": routes, "route_weights": route_weights, "expert_gate": expert_gate, "expert_up": expert_up, "expert_down": expert_down}


def ancestors(parents):
    tokens_per = parents.shape[1]
    position = jnp.arange(tokens_per, dtype=jnp.int32)
    identity = (position[:, None] == position[None, :]).astype(jnp.float32)
    linked = (parents[:, :, None] == position[None, None, :]) & (position[None, :, None] > 0)
    reached = jnp.maximum(identity[None], linked.astype(jnp.float32))
    for rounds in range(tokens_per.bit_length()):
        reached = jnp.minimum(jnp.einsum('bij,bjk->bik', reached, reached, precision=lax.Precision.HIGHEST), 1.0)
    return reached

def compact_path(reached, accepted, stacked):
    tokens_per = reached.shape[1]
    position = jnp.arange(tokens_per, dtype=jnp.int32)
    levels = lax.optimization_barrier(jnp.sum(reached, axis=2)) - 1.0
    leaf_row = (accepted[:, None] == position[None, :]).astype(jnp.float32)
    on_path = jnp.einsum('bi,bij->bj', leaf_row, reached, precision=lax.Precision.HIGHEST)
    chooser = on_path[:, None, :] * (levels[:, None, :] == position[None, :, None].astype(jnp.float32)).astype(jnp.float32)
    return jnp.einsum('btj,bjc->btc', chooser, stacked.astype(jnp.float32), precision=lax.Precision.HIGHEST).astype(jnp.bfloat16)

def attend(queries, cache_keys, cache_values, lengths, new_keys, new_values, reached):
    batch, tokens_per, width = queries.shape
    heads = width // HEAD
    scale = HEAD ** (-0.5)
    shape_q = (batch, tokens_per, heads, HEAD)
    shape_c = (batch, cache_keys.shape[1], heads, HEAD)
    query_four = queries.reshape(shape_q).astype(jnp.float32)
    cache_scores = jnp.einsum('bthe,blhe->bhtl', query_four, cache_keys.reshape(shape_c).astype(jnp.float32)) * scale
    valid = jnp.arange(cache_keys.shape[1], dtype=jnp.int32)[None, :] < lengths[:, None]
    cache_scores = jnp.where(valid[:, None, None, :], cache_scores, -jnp.inf)
    draft_scores = jnp.einsum('bthe,bshe->bhts', query_four, new_keys.reshape(shape_q).astype(jnp.float32)) * scale
    draft_scores = jnp.where(reached[:, None] > 0.5, draft_scores, -jnp.inf)
    highest = jnp.maximum(lax.optimization_barrier(jnp.max(cache_scores, axis=3)), lax.optimization_barrier(jnp.max(draft_scores, axis=3)))
    cache_probs = jnp.exp(cache_scores - highest[..., None])
    draft_probs = jnp.exp(draft_scores - highest[..., None])
    totals = lax.optimization_barrier(jnp.sum(cache_probs, axis=3)) + lax.optimization_barrier(jnp.sum(draft_probs, axis=3))
    cache_round = lax.optimization_barrier(cache_probs.astype(jnp.bfloat16)).astype(jnp.float32)
    draft_round = lax.optimization_barrier(draft_probs.astype(jnp.bfloat16)).astype(jnp.float32)
    mixed = jnp.einsum('bhtl,blhe->bthe', cache_round, cache_values.reshape(shape_c).astype(jnp.float32))
    mixed = mixed + jnp.einsum('bhts,bshe->bthe', draft_round, new_values.reshape(shape_q).astype(jnp.float32))
    mixed = mixed / jnp.transpose(totals, (0, 2, 1))[..., None]
    return mixed.reshape(batch, tokens_per, width).astype(jnp.bfloat16)

def single_request(item):
    return attend(*[member[None] for member in item])[0]

def reference(queries, new_keys, new_values, long_keys, long_values, long_lengths, short_keys, short_values, short_lengths, parents, accepted, residual, out_weight, norm_gain, routes, route_weights, expert_gate, expert_up, expert_down):
    reached = ancestors(parents)
    stacked = jnp.concatenate([new_keys, new_values], axis=2)
    compacted = compact_path(reached, accepted, stacked)
    accepted_keys = compacted[:, :, :HD]
    accepted_values = compacted[:, :, HD:]
    query_groups = queries.reshape(LONG, REQ_DEV, DRAFT, HD)
    key_groups = new_keys.reshape(LONG, REQ_DEV, DRAFT, HD)
    value_groups = new_values.reshape(LONG, REQ_DEV, DRAFT, HD)
    reach_groups = reached.reshape(LONG, REQ_DEV, DRAFT, DRAFT)
    long_items = (query_groups[:, 0], long_keys, long_values, long_lengths, key_groups[:, 0], value_groups[:, 0], reach_groups[:, 0])
    short_items = (query_groups[:, 1:].reshape(SHORT, DRAFT, HD), short_keys, short_values, short_lengths, key_groups[:, 1:].reshape(SHORT, DRAFT, HD), value_groups[:, 1:].reshape(SHORT, DRAFT, HD), reach_groups[:, 1:].reshape(SHORT, DRAFT, DRAFT))
    long_out = lax.map(single_request, long_items)
    short_out = lax.map(single_request, short_items)
    attended = jnp.concatenate([long_out[:, None], short_out.reshape(LONG, SHORT_DEV, DRAFT, HD)], axis=1).reshape(TOKENS, HD)
    attn_proj = jnp.dot(attended, out_weight, preferred_element_type=jnp.float32)
    middle = residual + attn_proj
    normed = (middle * lax.rsqrt(lax.optimization_barrier(jnp.mean(middle * middle, axis=1, keepdims=True)) + 1e-05) * norm_gain).astype(jnp.bfloat16)
    flat_routes = routes.reshape(-1)
    order = jnp.argsort(flat_routes, stable=True).astype(jnp.int32)
    sorted_experts = flat_routes[order]
    token_of = (order // TOPK).astype(jnp.int32)
    weight_of = route_weights.reshape(-1)[order]
    window = CAP * N_REQ * N_EXP
    starts = jnp.searchsorted(sorted_experts, jnp.arange(EXPERTS, dtype=jnp.int32)).astype(jnp.int32)
    token_pad = jnp.concatenate([token_of, jnp.zeros((window,), jnp.int32)])
    expert_pad = jnp.concatenate([sorted_experts, jnp.full((window,), EXPERTS, jnp.int32)])
    weight_pad = jnp.concatenate([weight_of, jnp.zeros((window,), jnp.float32)])

    def one_expert(carry, expert):
        begin = starts[expert]
        rows_index = lax.dynamic_slice_in_dim(token_pad, begin, window)
        owners = lax.dynamic_slice_in_dim(expert_pad, begin, window)
        weights_here = jnp.where(owners == expert, lax.dynamic_slice_in_dim(weight_pad, begin, window), 0.0)
        chosen = normed[rows_index]
        combined = jnp.zeros((window, D), jnp.float32)
        for piece in range(PIECES):
            index = expert * PIECES + piece
            gate_w = lax.dynamic_index_in_dim(expert_gate, index, 0, keepdims=False)
            up_w = lax.dynamic_index_in_dim(expert_up, index, 0, keepdims=False)
            down_w = lax.dynamic_index_in_dim(expert_down, index, 0, keepdims=False)
            gate_part = jnp.dot(chosen, gate_w, preferred_element_type=jnp.float32)
            up_part = jnp.dot(chosen, up_w, preferred_element_type=jnp.float32)
            activation = (jax.nn.silu(gate_part) * up_part).astype(jnp.bfloat16)
            piece_out = jnp.dot(activation, down_w, preferred_element_type=jnp.float32).astype(jnp.bfloat16)
            combined = combined + piece_out.astype(jnp.float32)
        return (carry.at[rows_index].add(weights_here[:, None] * combined), None)
    moe, _ = lax.scan(one_expert, jnp.zeros((TOKENS, D), jnp.float32), jnp.arange(EXPERTS, dtype=jnp.int32))
    hidden_out = (middle + moe).astype(jnp.bfloat16)
    return (hidden_out, accepted_keys, accepted_values)
```

```python
import jax
import jax.numpy as jnp
from jax import lax
from jax.sharding import PartitionSpec as P

HEAD = 128
EXPERTS = 64


def ancestors(parents):
    tokens_per = parents.shape[1]
    position = jnp.arange(tokens_per, dtype=jnp.int32)
    identity = (position[:, None] == position[None, :]).astype(jnp.float32)
    linked = (parents[:, :, None] == position[None, None, :]) & (position[None, :, None] > 0)
    reached = jnp.maximum(identity[None], linked.astype(jnp.float32))
    for rounds in range(tokens_per.bit_length()):
        reached = jnp.minimum(
            jnp.einsum("bij,bjk->bik", reached, reached, precision=lax.Precision.HIGHEST), 1.0
        )
    return reached


def compact_path(reached, accepted, stacked):
    tokens_per = reached.shape[1]
    position = jnp.arange(tokens_per, dtype=jnp.int32)
    levels = jnp.sum(reached, axis=2) - 1.0
    leaf_row = (accepted[:, None] == position[None, :]).astype(jnp.float32)
    on_path = jnp.einsum("bi,bij->bj", leaf_row, reached, precision=lax.Precision.HIGHEST)
    chooser = on_path[:, None, :] * (
        levels[:, None, :] == position[None, :, None].astype(jnp.float32)
    ).astype(jnp.float32)
    return jnp.einsum(
        "btj,bjc->btc", chooser.astype(jnp.bfloat16), stacked, preferred_element_type=jnp.float32
    ).astype(jnp.bfloat16)


def attend(queries, cache_keys, cache_values, lengths, new_keys, new_values, reached):
    batch, tokens_per, width = queries.shape
    heads = width // HEAD
    scale = HEAD ** (-0.5)
    shape_q = (batch, tokens_per, heads, HEAD)
    shape_c = (batch, cache_keys.shape[1], heads, HEAD)
    query_four = queries.reshape(shape_q)
    cache_scores = (
        jnp.einsum(
            "bthe,blhe->bhtl",
            query_four,
            cache_keys.reshape(shape_c),
            preferred_element_type=jnp.float32,
        )
        * scale
    )
    valid = jnp.arange(cache_keys.shape[1], dtype=jnp.int32)[None, :] < lengths[:, None]
    cache_scores = jnp.where(valid[:, None, None, :], cache_scores, -jnp.inf)
    draft_scores = (
        jnp.einsum(
            "bthe,bshe->bhts",
            query_four,
            new_keys.reshape(shape_q),
            preferred_element_type=jnp.float32,
        )
        * scale
    )
    draft_scores = jnp.where(reached[:, None] > 0.5, draft_scores, -jnp.inf)
    highest = jnp.maximum(jnp.max(cache_scores, axis=3), jnp.max(draft_scores, axis=3))
    cache_probs = jnp.exp(cache_scores - highest[..., None])
    draft_probs = jnp.exp(draft_scores - highest[..., None])
    totals = jnp.sum(cache_probs, axis=3) + jnp.sum(draft_probs, axis=3)
    mixed = jnp.einsum(
        "bhtl,blhe->bthe",
        cache_probs.astype(jnp.bfloat16),
        cache_values.reshape(shape_c),
        preferred_element_type=jnp.float32,
    )
    mixed = mixed + jnp.einsum(
        "bhts,bshe->bthe",
        draft_probs.astype(jnp.bfloat16),
        new_values.reshape(shape_q),
        preferred_element_type=jnp.float32,
    )
    mixed = mixed / jnp.transpose(totals, (0, 2, 1))[..., None]
    return mixed.reshape(batch, tokens_per, width).astype(jnp.bfloat16)


def expert_rows(rows, expert_gate, expert_up, expert_down):
    gate_part = jnp.dot(rows, expert_gate, preferred_element_type=jnp.float32)
    up_part = jnp.dot(rows, expert_up, preferred_element_type=jnp.float32)
    activation = (jax.nn.silu(gate_part) * up_part).astype(jnp.bfloat16)
    return jnp.dot(activation, expert_down, preferred_element_type=jnp.float32).astype(jnp.bfloat16)


def per_device(
    queries,
    new_keys,
    new_values,
    long_keys,
    long_values,
    long_lengths,
    short_keys,
    short_values,
    short_lengths,
    parents,
    accepted,
    residual,
    out_weight,
    norm_gain,
    routes,
    route_weights,
    expert_gate,
    expert_up,
    expert_down,
):
    reached = ancestors(parents)
    head_width = new_keys.shape[2]
    stacked = jnp.concatenate([new_keys, new_values], axis=2)
    compacted = compact_path(reached, accepted, stacked)
    accepted_keys = compacted[:, :, :head_width]
    accepted_values = compacted[:, :, head_width:]
    long_out = attend(
        queries[:1], long_keys, long_values, long_lengths, new_keys[:1], new_values[:1], reached[:1]
    )
    short_out = attend(
        queries[1:],
        short_keys,
        short_values,
        short_lengths,
        new_keys[1:],
        new_values[1:],
        reached[1:],
    )
    attended = jnp.concatenate([long_out, short_out], axis=0).reshape(-1, head_width)
    n_exp = lax.axis_size("exp")
    model_width = out_weight.shape[1]
    partial = jnp.dot(attended, out_weight, preferred_element_type=jnp.float32).astype(jnp.bfloat16)
    partial = partial.reshape(n_exp, -1, model_width)
    gathered = lax.all_to_all(partial, "exp", split_axis=0, concat_axis=0, tiled=True)
    attn_proj = jnp.sum(gathered.astype(jnp.float32), axis=0)
    middle = residual + attn_proj
    normed = (
        middle * lax.rsqrt(jnp.mean(middle * middle, axis=1, keepdims=True) + 1e-05) * norm_gain
    ).astype(jnp.bfloat16)
    tok_rows, top_count = routes.shape
    devices = lax.axis_size("req") * lax.axis_size("exp")
    pieces = max(1, devices // EXPERTS)
    capacity = 2 * tok_rows * top_count // EXPERTS
    flat_routes = routes.reshape(-1)
    flat_count = flat_routes.shape[0]
    expert_ids = jnp.arange(EXPERTS, dtype=jnp.int32)
    onehot = (flat_routes[:, None] == expert_ids[None, :]).astype(jnp.float32)
    flat_ids = jnp.arange(flat_count, dtype=jnp.int32)
    earlier = (flat_ids[:, None] > flat_ids[None, :]).astype(jnp.float32)
    before = jnp.dot(earlier, onehot, precision=lax.Precision.HIGHEST)
    slot_index = jnp.sum(before * onehot, axis=1).astype(jnp.int32).reshape(tok_rows, top_count)
    target = routes * capacity + slot_index
    columns = jnp.arange(EXPERTS * pieces * capacity, dtype=jnp.int32)
    column_target = (columns // (pieces * capacity)) * capacity + columns % capacity
    hits = target[:, :, None] == column_target[None, None, :]
    placement = jnp.any(hits, axis=1).astype(jnp.bfloat16)
    packed = jnp.einsum("tc,td->cd", placement, normed, preferred_element_type=jnp.float32).astype(
        jnp.bfloat16
    )
    outgoing = packed.reshape(devices, capacity, model_width)
    received = lax.all_to_all(outgoing, ("req", "exp"), split_axis=0, concat_axis=0, tiled=True)
    produced = expert_rows(
        received.reshape(-1, model_width), expert_gate[0], expert_up[0], expert_down[0]
    ).reshape(devices, capacity, model_width)
    returned = lax.all_to_all(produced, ("req", "exp"), split_axis=0, concat_axis=0, tiled=True)
    chooser = hits.reshape(tok_rows * top_count, -1).astype(jnp.bfloat16)
    expert_out = jnp.dot(
        chooser, returned.reshape(-1, model_width), preferred_element_type=jnp.float32
    ).reshape(tok_rows, top_count, model_width)
    moe = jnp.sum(route_weights[:, :, None] * expert_out, axis=1)
    hidden_out = (middle + moe).astype(jnp.bfloat16)
    return (hidden_out, accepted_keys, accepted_values)


def solution(mesh):
    in_specs = (
        P("req", None, "exp"),
        P("req", None, "exp"),
        P("req", None, "exp"),
        P("req", None, "exp"),
        P("req", None, "exp"),
        P("req"),
        P("req", None, "exp"),
        P("req", None, "exp"),
        P("req"),
        P("req", None),
        P("req"),
        P(("req", "exp"), None),
        P("exp", None),
        P(),
        P(("req", "exp"), None),
        P(("req", "exp"), None),
        P(("req", "exp"), None, None),
        P(("req", "exp"), None, None),
        P(("req", "exp"), None, None),
    )
    out_specs = (P(("req", "exp"), None), P("req", None, "exp"), P("req", None, "exp"))
    return jax.shard_map(
        per_device, mesh=mesh, in_specs=in_specs, out_specs=out_specs, check_vma=False
    )
```

```python
import jax
import jax.numpy as jnp
from jax import lax
from jax.sharding import PartitionSpec as P

HEAD = 128
EXPERTS = 64


def ancestors(parents):
    tokens_per = parents.shape[1]
    position = jnp.arange(tokens_per, dtype=jnp.int32)
    identity = (position[:, None] == position[None, :]).astype(jnp.float32)
    linked = (parents[:, :, None] == position[None, None, :]) & (position[None, :, None] > 0)
    reached = jnp.maximum(identity[None], linked.astype(jnp.float32))
    for rounds in range(tokens_per.bit_length()):
        reached = jnp.minimum(
            jnp.einsum("bij,bjk->bik", reached, reached, precision=lax.Precision.HIGHEST), 1.0
        )
    return reached


def compact_path(reached, accepted, stacked):
    tokens_per = reached.shape[1]
    position = jnp.arange(tokens_per, dtype=jnp.int32)
    levels = jnp.sum(reached, axis=2) - 1.0
    leaf_row = (accepted[:, None] == position[None, :]).astype(jnp.float32)
    on_path = jnp.einsum("bi,bij->bj", leaf_row, reached, precision=lax.Precision.HIGHEST)
    chooser = on_path[:, None, :] * (
        levels[:, None, :] == position[None, :, None].astype(jnp.float32)
    ).astype(jnp.float32)
    return jnp.einsum(
        "btj,bjc->btc", chooser.astype(jnp.bfloat16), stacked, preferred_element_type=jnp.float32
    ).astype(jnp.bfloat16)


def attend(queries, cache_keys, cache_values, lengths, new_keys, new_values, reached):
    batch, tokens_per, width = queries.shape
    heads = width // HEAD
    scale = HEAD ** (-0.5)
    shape_q = (batch, tokens_per, heads, HEAD)
    shape_n = (batch, new_keys.shape[1], heads, HEAD)
    shape_c = (batch, cache_keys.shape[1], heads, HEAD)
    query_four = queries.reshape(shape_q)
    cache_scores = (
        jnp.einsum(
            "bthe,blhe->bhtl",
            query_four,
            cache_keys.reshape(shape_c),
            preferred_element_type=jnp.float32,
        )
        * scale
    )
    valid = jnp.arange(cache_keys.shape[1], dtype=jnp.int32)[None, :] < lengths[:, None]
    cache_scores = jnp.where(valid[:, None, None, :], cache_scores, -jnp.inf)
    draft_scores = (
        jnp.einsum(
            "bthe,bshe->bhts",
            query_four,
            new_keys.reshape(shape_n),
            preferred_element_type=jnp.float32,
        )
        * scale
    )
    draft_scores = jnp.where(reached[:, None] > 0.5, draft_scores, -jnp.inf)
    highest = jnp.maximum(jnp.max(cache_scores, axis=3), jnp.max(draft_scores, axis=3))
    cache_probs = jnp.exp(cache_scores - highest[..., None])
    draft_probs = jnp.exp(draft_scores - highest[..., None])
    totals = jnp.sum(cache_probs, axis=3) + jnp.sum(draft_probs, axis=3)
    mixed = jnp.einsum(
        "bhtl,blhe->bthe",
        cache_probs.astype(jnp.bfloat16),
        cache_values.reshape(shape_c),
        preferred_element_type=jnp.float32,
    )
    mixed = mixed + jnp.einsum(
        "bhts,bshe->bthe",
        draft_probs.astype(jnp.bfloat16),
        new_values.reshape(shape_n),
        preferred_element_type=jnp.float32,
    )
    mixed = mixed / jnp.transpose(totals, (0, 2, 1))[..., None]
    return mixed.reshape(batch, tokens_per, width).astype(jnp.bfloat16)


def expert_rows(rows, expert_gate, expert_up, expert_down):
    gate_part = jnp.dot(rows, expert_gate, preferred_element_type=jnp.float32)
    up_part = jnp.dot(rows, expert_up, preferred_element_type=jnp.float32)
    activation = (jax.nn.silu(gate_part) * up_part).astype(jnp.bfloat16)
    return jnp.dot(activation, expert_down, preferred_element_type=jnp.float32).astype(jnp.bfloat16)


def per_device(
    queries,
    new_keys,
    new_values,
    long_keys,
    long_values,
    long_lengths,
    short_keys,
    short_values,
    short_lengths,
    parents,
    accepted,
    residual,
    out_weight,
    norm_gain,
    routes,
    route_weights,
    expert_gate,
    expert_up,
    expert_down,
):
    reached = ancestors(parents)
    head_width = new_keys.shape[2]
    stacked = jnp.concatenate([new_keys, new_values], axis=2)
    compacted = compact_path(reached, accepted, stacked)
    accepted_keys = compacted[:, :, :head_width]
    accepted_values = compacted[:, :, head_width:]
    n_exp = lax.axis_size("exp")
    model_width = out_weight.shape[1]
    halves = 2
    q_rows = queries.shape[1] // halves
    exchanged = []
    for half in range(halves):
        rows = slice(half * q_rows, (half + 1) * q_rows)
        long_out = attend(
            queries[:1, rows],
            long_keys,
            long_values,
            long_lengths,
            new_keys[:1],
            new_values[:1],
            reached[:1, rows],
        )
        short_out = attend(
            queries[1:, rows],
            short_keys,
            short_values,
            short_lengths,
            new_keys[1:],
            new_values[1:],
            reached[1:, rows],
        )
        attended = jnp.concatenate([long_out, short_out], axis=0).reshape(-1, head_width)
        partial = jnp.dot(attended, out_weight, preferred_element_type=jnp.float32)
        partial = partial.astype(jnp.bfloat16).reshape(n_exp, q_rows, model_width)
        exchanged.append(lax.all_to_all(partial, "exp", split_axis=0, concat_axis=0, tiled=True))
    gathered = jnp.concatenate(exchanged, axis=1)
    attn_proj = jnp.sum(gathered.astype(jnp.float32), axis=0)
    middle = residual + attn_proj
    normed = (
        middle * lax.rsqrt(jnp.mean(middle * middle, axis=1, keepdims=True) + 1e-05) * norm_gain
    ).astype(jnp.bfloat16)
    tok_rows, top_count = routes.shape
    devices = lax.axis_size("req") * lax.axis_size("exp")
    pieces = max(1, devices // EXPERTS)
    capacity = 2 * tok_rows * top_count // EXPERTS
    flat_routes = routes.reshape(-1)
    flat_count = flat_routes.shape[0]
    expert_ids = jnp.arange(EXPERTS, dtype=jnp.int32)
    onehot = (flat_routes[:, None] == expert_ids[None, :]).astype(jnp.float32)
    flat_ids = jnp.arange(flat_count, dtype=jnp.int32)
    earlier = (flat_ids[:, None] > flat_ids[None, :]).astype(jnp.float32)
    before = jnp.dot(earlier, onehot, precision=lax.Precision.HIGHEST)
    slot_index = jnp.sum(before * onehot, axis=1).astype(jnp.int32).reshape(tok_rows, top_count)
    target = routes * capacity + slot_index
    columns = jnp.arange(EXPERTS * pieces * capacity, dtype=jnp.int32)
    column_target = (columns // (pieces * capacity)) * capacity + columns % capacity
    hits = (target[:, :, None] == column_target[None, None, :]).reshape(
        tok_rows, top_count, devices, capacity
    )
    placement = jnp.any(hits, axis=1).astype(jnp.bfloat16)
    chooser = hits.reshape(tok_rows * top_count, devices, capacity).astype(jnp.bfloat16)
    chunks = 2
    chunk_slots = capacity // chunks
    expert_out = None
    for chunk in range(chunks):
        slots = slice(chunk * chunk_slots, (chunk + 1) * chunk_slots)
        packed = jnp.einsum(
            "tc,td->cd",
            placement[:, :, slots].reshape(tok_rows, -1),
            normed,
            preferred_element_type=jnp.float32,
        ).astype(jnp.bfloat16)
        outgoing = packed.reshape(devices, chunk_slots, model_width)
        received = lax.all_to_all(outgoing, ("req", "exp"), split_axis=0, concat_axis=0, tiled=True)
        produced = expert_rows(
            received.reshape(-1, model_width), expert_gate[0], expert_up[0], expert_down[0]
        ).reshape(devices, chunk_slots, model_width)
        returned = lax.all_to_all(produced, ("req", "exp"), split_axis=0, concat_axis=0, tiled=True)
        part = jnp.dot(
            chooser[:, :, slots].reshape(tok_rows * top_count, -1),
            returned.reshape(-1, model_width),
            preferred_element_type=jnp.float32,
        )
        expert_out = part if expert_out is None else expert_out + part
    expert_out = expert_out.reshape(tok_rows, top_count, model_width)
    moe = jnp.sum(route_weights[:, :, None] * expert_out, axis=1)
    hidden_out = (middle + moe).astype(jnp.bfloat16)
    return (hidden_out, accepted_keys, accepted_values)


def solution(mesh):
    in_specs = (
        P("req", None, "exp"),
        P("req", None, "exp"),
        P("req", None, "exp"),
        P("req", None, "exp"),
        P("req", None, "exp"),
        P("req"),
        P("req", None, "exp"),
        P("req", None, "exp"),
        P("req"),
        P("req", None),
        P("req"),
        P(("req", "exp"), None),
        P("exp", None),
        P(),
        P(("req", "exp"), None),
        P(("req", "exp"), None),
        P(("req", "exp"), None, None),
        P(("req", "exp"), None, None),
        P(("req", "exp"), None, None),
    )
    out_specs = (P(("req", "exp"), None), P("req", None, "exp"), P("req", None, "exp"))
    return jax.shard_map(
        per_device, mesh=mesh, in_specs=in_specs, out_specs=out_specs, check_vma=False
    )
```

```python
import jax
import jax.numpy as jnp
from jax import lax
from jax.sharding import PartitionSpec as P

HEAD = 128
EXPERTS = 64


def ancestors(parents):
    tokens_per = parents.shape[1]
    position = jnp.arange(tokens_per, dtype=jnp.int32)
    identity = (position[:, None] == position[None, :]).astype(jnp.float32)
    linked = (parents[:, :, None] == position[None, None, :]) & (position[None, :, None] > 0)
    reached = jnp.maximum(identity[None], linked.astype(jnp.float32))
    for rounds in range(tokens_per.bit_length()):
        squared = reached.astype(jnp.bfloat16)
        reached = jnp.minimum(
            jnp.einsum("bij,bjk->bik", squared, squared, preferred_element_type=jnp.float32), 1.0
        )
    return reached


def compact_path(reached, accepted, stacked):
    tokens_per = reached.shape[1]
    position = jnp.arange(tokens_per, dtype=jnp.int32)
    levels = jnp.sum(reached, axis=2) - 1.0
    leaf_row = (accepted[:, None] == position[None, :]).astype(jnp.float32)
    on_path = jnp.einsum(
        "bi,bij->bj",
        leaf_row.astype(jnp.bfloat16),
        reached.astype(jnp.bfloat16),
        preferred_element_type=jnp.float32,
    )
    chooser = on_path[:, None, :] * (
        levels[:, None, :] == position[None, :, None].astype(jnp.float32)
    ).astype(jnp.float32)
    return jnp.einsum(
        "btj,bjc->btc", chooser.astype(jnp.bfloat16), stacked, preferred_element_type=jnp.float32
    ).astype(jnp.bfloat16)


def attend(queries, cache_keys, cache_values, lengths, new_keys, new_values, reached):
    batch, tokens_per, width = queries.shape
    heads = width // HEAD
    scale = HEAD ** (-0.5)
    shape_q = (batch, tokens_per, heads, HEAD)
    shape_c = (batch, cache_keys.shape[1], heads, HEAD)
    query_four = queries.reshape(shape_q)
    cache_scores = (
        jnp.einsum(
            "bthe,blhe->bhtl",
            query_four,
            cache_keys.reshape(shape_c),
            preferred_element_type=jnp.float32,
        )
        * scale
    )
    valid = jnp.arange(cache_keys.shape[1], dtype=jnp.int32)[None, :] < lengths[:, None]
    cache_scores = jnp.where(valid[:, None, None, :], cache_scores, -jnp.inf)
    draft_scores = (
        jnp.einsum(
            "bthe,bshe->bhts",
            query_four,
            new_keys.reshape(shape_q),
            preferred_element_type=jnp.float32,
        )
        * scale
    )
    draft_scores = jnp.where(reached[:, None] > 0.5, draft_scores, -jnp.inf)
    highest = jnp.maximum(jnp.max(cache_scores, axis=3), jnp.max(draft_scores, axis=3))
    cache_probs = jnp.exp(cache_scores - highest[..., None])
    draft_probs = jnp.exp(draft_scores - highest[..., None])
    totals = jnp.sum(cache_probs, axis=3) + jnp.sum(draft_probs, axis=3)
    mixed = jnp.einsum(
        "bhtl,blhe->bthe",
        cache_probs.astype(jnp.bfloat16),
        cache_values.reshape(shape_c),
        preferred_element_type=jnp.float32,
    )
    mixed = mixed + jnp.einsum(
        "bhts,bshe->bthe",
        draft_probs.astype(jnp.bfloat16),
        new_values.reshape(shape_q),
        preferred_element_type=jnp.float32,
    )
    mixed = mixed / jnp.transpose(totals, (0, 2, 1))[..., None]
    return mixed.reshape(batch, tokens_per, width).astype(jnp.bfloat16)


def expert_rows(rows, expert_gate, expert_up, expert_down):
    gate_part = jnp.dot(rows, expert_gate, preferred_element_type=jnp.float32)
    up_part = jnp.dot(rows, expert_up, preferred_element_type=jnp.float32)
    activation = (jax.nn.silu(gate_part) * up_part).astype(jnp.bfloat16)
    return jnp.dot(activation, expert_down, preferred_element_type=jnp.float32).astype(jnp.bfloat16)


def per_device(
    queries,
    new_keys,
    new_values,
    long_keys,
    long_values,
    long_lengths,
    short_keys,
    short_values,
    short_lengths,
    parents,
    accepted,
    residual,
    out_weight,
    norm_gain,
    routes,
    route_weights,
    expert_gate,
    expert_up,
    expert_down,
):
    reached = ancestors(parents)
    head_width = new_keys.shape[2]
    stacked = jnp.concatenate([new_keys, new_values], axis=2)
    compacted = compact_path(reached, accepted, stacked)
    accepted_keys = compacted[:, :, :head_width]
    accepted_values = compacted[:, :, head_width:]
    long_out = attend(
        queries[:1], long_keys, long_values, long_lengths, new_keys[:1], new_values[:1], reached[:1]
    )
    short_out = attend(
        queries[1:],
        short_keys,
        short_values,
        short_lengths,
        new_keys[1:],
        new_values[1:],
        reached[1:],
    )
    attended = jnp.concatenate([long_out, short_out], axis=0).reshape(-1, head_width)
    n_exp = lax.axis_size("exp")
    model_width = out_weight.shape[1]
    split = model_width // 2
    swapped = jnp.dot(attended, out_weight[:, :split], preferred_element_type=jnp.float32)
    reduced = jnp.dot(attended, out_weight[:, split:], preferred_element_type=jnp.float32)
    reduced = lax.psum_scatter(
        reduced.astype(jnp.bfloat16), "exp", scatter_dimension=0, tiled=True
    )
    swapped = swapped.astype(jnp.bfloat16).reshape(n_exp, -1, split)
    gathered = lax.all_to_all(swapped, "exp", split_axis=0, concat_axis=0, tiled=True)
    attn_proj = jnp.concatenate(
        [jnp.sum(gathered.astype(jnp.float32), axis=0), reduced.astype(jnp.float32)], axis=1
    )
    middle = residual + attn_proj
    normed = (
        middle * lax.rsqrt(jnp.mean(middle * middle, axis=1, keepdims=True) + 1e-05) * norm_gain
    ).astype(jnp.bfloat16)
    tok_rows, top_count = routes.shape
    devices = lax.axis_size("req") * lax.axis_size("exp")
    pieces = max(1, devices // EXPERTS)
    capacity = 2 * tok_rows * top_count // EXPERTS
    flat_routes = routes.reshape(-1)
    flat_count = flat_routes.shape[0]
    expert_ids = jnp.arange(EXPERTS, dtype=jnp.int32)
    onehot = (flat_routes[:, None] == expert_ids[None, :]).astype(jnp.float32)
    flat_ids = jnp.arange(flat_count, dtype=jnp.int32)
    earlier = (flat_ids[:, None] > flat_ids[None, :]).astype(jnp.float32)
    before = jnp.dot(earlier, onehot, precision=lax.Precision.HIGHEST)
    slot_index = jnp.sum(before * onehot, axis=1).astype(jnp.int32).reshape(tok_rows, top_count)
    target = routes * capacity + slot_index
    columns = jnp.arange(EXPERTS * pieces * capacity, dtype=jnp.int32)
    column_target = (columns // (pieces * capacity)) * capacity + columns % capacity
    hits = target[:, :, None] == column_target[None, None, :]
    placement = jnp.any(hits, axis=1).astype(jnp.bfloat16)
    packed = jnp.einsum("tc,td->cd", placement, normed, preferred_element_type=jnp.float32).astype(
        jnp.bfloat16
    )
    outgoing = packed.reshape(devices, capacity, model_width)
    received = lax.all_to_all(outgoing, ("req", "exp"), split_axis=0, concat_axis=0, tiled=True)
    produced = expert_rows(
        received.reshape(-1, model_width), expert_gate[0], expert_up[0], expert_down[0]
    ).reshape(devices, capacity, model_width)
    returned = lax.all_to_all(produced, ("req", "exp"), split_axis=0, concat_axis=0, tiled=True)
    weighing = jnp.sum(jnp.where(hits, route_weights[:, :, None], 0.0), axis=1)
    terms = []
    for _ in range(3):
        term = weighing.astype(jnp.bfloat16)
        terms.append(term)
        weighing = weighing - term.astype(jnp.float32)
    terms = jnp.concatenate(terms, axis=0)
    moe = jnp.dot(terms, returned.reshape(-1, model_width), preferred_element_type=jnp.float32)
    moe = jnp.sum(moe.reshape(3, tok_rows, model_width), axis=0)
    hidden_out = (middle + moe).astype(jnp.bfloat16)
    return (hidden_out, accepted_keys, accepted_values)


def solution(mesh):
    in_specs = (
        P("req", None, "exp"),
        P("req", None, "exp"),
        P("req", None, "exp"),
        P("req", None, "exp"),
        P("req", None, "exp"),
        P("req"),
        P("req", None, "exp"),
        P("req", None, "exp"),
        P("req"),
        P("req", None),
        P("req"),
        P(("req", "exp"), None),
        P("exp", None),
        P(),
        P(("req", "exp"), None),
        P(("req", "exp"), None),
        P(("req", "exp"), None, None),
        P(("req", "exp"), None, None),
        P(("req", "exp"), None, None),
    )
    out_specs = (P(("req", "exp"), None), P("req", None, "exp"), P("req", None, "exp"))
    return jax.shard_map(
        per_device, mesh=mesh, in_specs=in_specs, out_specs=out_specs, check_vma=False
    )
```

```python
import jax
import jax.numpy as jnp
from jax import lax
from jax.sharding import PartitionSpec as P

HEAD = 128
EXPERTS = 64


def ancestors(parents):
    tokens_per = parents.shape[1]
    position = jnp.arange(tokens_per, dtype=jnp.int32)
    identity = (position[:, None] == position[None, :]).astype(jnp.float32)
    linked = (parents[:, :, None] == position[None, None, :]) & (position[None, :, None] > 0)
    reached = jnp.maximum(identity[None], linked.astype(jnp.float32))
    for rounds in range(tokens_per.bit_length()):
        squared = reached.astype(jnp.bfloat16)
        reached = jnp.minimum(
            jnp.einsum("bij,bjk->bik", squared, squared, preferred_element_type=jnp.float32), 1.0
        )
    return reached


def compact_path(reached, accepted, stacked):
    tokens_per = reached.shape[1]
    position = jnp.arange(tokens_per, dtype=jnp.int32)
    levels = jnp.sum(reached, axis=2) - 1.0
    leaf_row = (accepted[:, None] == position[None, :]).astype(jnp.float32)
    on_path = jnp.einsum(
        "bi,bij->bj",
        leaf_row.astype(jnp.bfloat16),
        reached.astype(jnp.bfloat16),
        preferred_element_type=jnp.float32,
    )
    chooser = on_path[:, None, :] * (
        levels[:, None, :] == position[None, :, None].astype(jnp.float32)
    ).astype(jnp.float32)
    return jnp.einsum(
        "btj,bjc->btc", chooser.astype(jnp.bfloat16), stacked, preferred_element_type=jnp.float32
    ).astype(jnp.bfloat16)


def attend(queries, cache_keys, cache_values, lengths, new_keys, new_values, reached):
    batch, tokens_per, width = queries.shape
    heads = width // HEAD
    scale = HEAD ** (-0.5)
    shape_q = (batch, tokens_per, heads, HEAD)
    shape_c = (batch, cache_keys.shape[1], heads, HEAD)
    query_four = queries.reshape(shape_q)
    cache_scores = (
        jnp.einsum(
            "bthe,blhe->bhtl",
            query_four,
            cache_keys.reshape(shape_c),
            preferred_element_type=jnp.float32,
        )
        * scale
    )
    valid = jnp.arange(cache_keys.shape[1], dtype=jnp.int32)[None, :] < lengths[:, None]
    cache_scores = jnp.where(valid[:, None, None, :], cache_scores, -jnp.inf)
    draft_scores = (
        jnp.einsum(
            "bthe,bshe->bhts",
            query_four,
            new_keys.reshape(shape_q),
            preferred_element_type=jnp.float32,
        )
        * scale
    )
    draft_scores = jnp.where(reached[:, None] > 0.5, draft_scores, -jnp.inf)
    highest = jnp.maximum(jnp.max(cache_scores, axis=3), jnp.max(draft_scores, axis=3))
    cache_probs = jnp.exp(cache_scores - highest[..., None])
    draft_probs = jnp.exp(draft_scores - highest[..., None])
    totals = jnp.sum(cache_probs, axis=3) + jnp.sum(draft_probs, axis=3)
    mixed = jnp.einsum(
        "bhtl,blhe->bthe",
        cache_probs.astype(jnp.bfloat16),
        cache_values.reshape(shape_c),
        preferred_element_type=jnp.float32,
    )
    mixed = mixed + jnp.einsum(
        "bhts,bshe->bthe",
        draft_probs.astype(jnp.bfloat16),
        new_values.reshape(shape_q),
        preferred_element_type=jnp.float32,
    )
    mixed = mixed / jnp.transpose(totals, (0, 2, 1))[..., None]
    return mixed.reshape(batch, tokens_per, width).astype(jnp.bfloat16)


def expert_rows(rows, expert_gate, expert_up, expert_down):
    gate_part = jnp.dot(rows, expert_gate, preferred_element_type=jnp.float32)
    up_part = jnp.dot(rows, expert_up, preferred_element_type=jnp.float32)
    activation = (jax.nn.silu(gate_part) * up_part).astype(jnp.bfloat16)
    return jnp.dot(activation, expert_down, preferred_element_type=jnp.float32).astype(jnp.bfloat16)


def ring_exchange(blocks, axis, forward, backward, own):
    ring = blocks.shape[0]
    rows = blocks.shape[1]
    half = rows // 2
    pick = lambda step: lax.dynamic_index_in_dim(blocks, (own + step) % ring, 0, keepdims=False)
    across = pick(2)
    to_right = jnp.concatenate([pick(1), across[:half]], axis=0)
    to_left = jnp.concatenate([pick(3), across[half:]], axis=0)
    from_left = lax.ppermute(to_right, axis, forward)
    from_right = lax.ppermute(to_left, axis, backward)
    far_left = lax.ppermute(from_left[rows:], axis, forward)
    far_right = lax.ppermute(from_right[rows:], axis, backward)
    total = pick(0).astype(jnp.float32) + from_left[:rows].astype(jnp.float32)
    total = total + from_right[:rows].astype(jnp.float32)
    return total + jnp.concatenate([far_left, far_right], axis=0).astype(jnp.float32)


def ring_reduce_scatter(attended, out_weight, n_exp):
    side = 4
    assert n_exp == side * side
    index = lax.axis_index("exp")
    z_pos, x_pos = index // side, index % side
    cells = [(z, x) for z in range(side) for x in range(side)]
    x_next = [(z * side + x, z * side + (x + 1) % side) for z, x in cells]
    x_prev = [(z * side + x, z * side + (x - 1) % side) for z, x in cells]
    z_next = [(z * side + x, ((z + 1) % side) * side + x) for z, x in cells]
    z_prev = [(z * side + x, ((z - 1) % side) * side + x) for z, x in cells]
    rows = attended.shape[0] // n_exp
    width = out_weight.shape[1]
    split = width // 2
    grid = attended.reshape(side, side, rows, -1)
    by_x = jnp.swapaxes(grid, 0, 1).reshape(n_exp * rows, -1)
    first = jnp.dot(by_x, out_weight[:, :split], preferred_element_type=jnp.float32)
    first = first.astype(jnp.bfloat16).reshape(side, side * rows, split)
    second = jnp.dot(attended, out_weight[:, split:], preferred_element_type=jnp.float32)
    second = second.astype(jnp.bfloat16).reshape(side, side * rows, split)
    first = ring_exchange(first, "exp", x_next, x_prev, x_pos)
    second = ring_exchange(second, "exp", z_next, z_prev, z_pos)
    first = ring_exchange(
        first.astype(jnp.bfloat16).reshape(side, rows, split), "exp", z_next, z_prev, z_pos
    )
    second = ring_exchange(
        second.astype(jnp.bfloat16).reshape(side, rows, split), "exp", x_next, x_prev, x_pos
    )
    return jnp.concatenate([first, second], axis=1)


def per_device(
    queries,
    new_keys,
    new_values,
    long_keys,
    long_values,
    long_lengths,
    short_keys,
    short_values,
    short_lengths,
    parents,
    accepted,
    residual,
    out_weight,
    norm_gain,
    routes,
    route_weights,
    expert_gate,
    expert_up,
    expert_down,
):
    reached = ancestors(parents)
    head_width = new_keys.shape[2]
    stacked = jnp.concatenate([new_keys, new_values], axis=2)
    compacted = compact_path(reached, accepted, stacked)
    accepted_keys = compacted[:, :, :head_width]
    accepted_values = compacted[:, :, head_width:]
    long_out = attend(
        queries[:1], long_keys, long_values, long_lengths, new_keys[:1], new_values[:1], reached[:1]
    )
    short_out = attend(
        queries[1:],
        short_keys,
        short_values,
        short_lengths,
        new_keys[1:],
        new_values[1:],
        reached[1:],
    )
    attended = jnp.concatenate([long_out, short_out], axis=0).reshape(-1, head_width)
    n_exp = lax.axis_size("exp")
    model_width = out_weight.shape[1]
    attn_proj = ring_reduce_scatter(attended, out_weight, n_exp)
    middle = residual + attn_proj
    normed = (
        middle * lax.rsqrt(jnp.mean(middle * middle, axis=1, keepdims=True) + 1e-05) * norm_gain
    ).astype(jnp.bfloat16)
    tok_rows, top_count = routes.shape
    devices = lax.axis_size("req") * lax.axis_size("exp")
    pieces = max(1, devices // EXPERTS)
    capacity = 2 * tok_rows * top_count // EXPERTS
    flat_routes = routes.reshape(-1)
    flat_count = flat_routes.shape[0]
    expert_ids = jnp.arange(EXPERTS, dtype=jnp.int32)
    onehot = (flat_routes[:, None] == expert_ids[None, :]).astype(jnp.float32)
    flat_ids = jnp.arange(flat_count, dtype=jnp.int32)
    earlier = (flat_ids[:, None] > flat_ids[None, :]).astype(jnp.float32)
    before = jnp.dot(earlier, onehot, precision=lax.Precision.HIGHEST)
    slot_index = jnp.sum(before * onehot, axis=1).astype(jnp.int32).reshape(tok_rows, top_count)
    target = routes * capacity + slot_index
    columns = jnp.arange(EXPERTS * pieces * capacity, dtype=jnp.int32)
    column_target = (columns // (pieces * capacity)) * capacity + columns % capacity
    hits = target[:, :, None] == column_target[None, None, :]
    placement = jnp.any(hits, axis=1).astype(jnp.bfloat16)
    packed = jnp.einsum("tc,td->cd", placement, normed, preferred_element_type=jnp.float32).astype(
        jnp.bfloat16
    )
    outgoing = packed.reshape(devices, capacity, model_width)
    received = lax.all_to_all(outgoing, ("req", "exp"), split_axis=0, concat_axis=0, tiled=True)
    produced = expert_rows(
        received.reshape(-1, model_width), expert_gate[0], expert_up[0], expert_down[0]
    ).reshape(devices, capacity, model_width)
    returned = lax.all_to_all(produced, ("req", "exp"), split_axis=0, concat_axis=0, tiled=True)
    weighing = jnp.sum(jnp.where(hits, route_weights[:, :, None], 0.0), axis=1)
    terms = []
    for _ in range(3):
        term = weighing.astype(jnp.bfloat16)
        terms.append(term)
        weighing = weighing - term.astype(jnp.float32)
    terms = jnp.concatenate(terms, axis=0)
    moe = jnp.dot(terms, returned.reshape(-1, model_width), preferred_element_type=jnp.float32)
    moe = jnp.sum(moe.reshape(3, tok_rows, model_width), axis=0)
    hidden_out = (middle + moe).astype(jnp.bfloat16)
    return (hidden_out, accepted_keys, accepted_values)


def solution(mesh):
    in_specs = (
        P("req", None, "exp"),
        P("req", None, "exp"),
        P("req", None, "exp"),
        P("req", None, "exp"),
        P("req", None, "exp"),
        P("req"),
        P("req", None, "exp"),
        P("req", None, "exp"),
        P("req"),
        P("req", None),
        P("req"),
        P(("req", "exp"), None),
        P("exp", None),
        P(),
        P(("req", "exp"), None),
        P(("req", "exp"), None),
        P(("req", "exp"), None, None),
        P(("req", "exp"), None, None),
        P(("req", "exp"), None, None),
    )
    out_specs = (P(("req", "exp"), None), P("req", None, "exp"), P("req", None, "exp"))
    return jax.shard_map(
        per_device, mesh=mesh, in_specs=in_specs, out_specs=out_specs, check_vma=False
    )
```

```python
import jax
import jax.numpy as jnp
from jax import lax
from jax.sharding import PartitionSpec as P

HEAD = 128
EXPERTS = 64


def ancestors(parents):
    tokens_per = parents.shape[1]
    position = jnp.arange(tokens_per, dtype=jnp.int32)
    identity = (position[:, None] == position[None, :]).astype(jnp.float32)
    linked = (parents[:, :, None] == position[None, None, :]) & (position[None, :, None] > 0)
    reached = jnp.maximum(identity[None], linked.astype(jnp.float32))
    for rounds in range(tokens_per.bit_length()):
        squared = reached.astype(jnp.bfloat16)
        reached = jnp.minimum(
            jnp.einsum("bij,bjk->bik", squared, squared, preferred_element_type=jnp.float32), 1.0
        )
    return reached


def compact_path(reached, accepted, stacked):
    tokens_per = reached.shape[1]
    position = jnp.arange(tokens_per, dtype=jnp.int32)
    levels = jnp.sum(reached, axis=2) - 1.0
    leaf_row = (accepted[:, None] == position[None, :]).astype(jnp.float32)
    on_path = jnp.einsum(
        "bi,bij->bj",
        leaf_row.astype(jnp.bfloat16),
        reached.astype(jnp.bfloat16),
        preferred_element_type=jnp.float32,
    )
    chooser = on_path[:, None, :] * (
        levels[:, None, :] == position[None, :, None].astype(jnp.float32)
    ).astype(jnp.float32)
    return jnp.einsum(
        "btj,bjc->btc", chooser.astype(jnp.bfloat16), stacked, preferred_element_type=jnp.float32
    ).astype(jnp.bfloat16)


def attend(queries, cache_keys, cache_values, lengths, new_keys, new_values, reached):
    batch, tokens_per, width = queries.shape
    heads = width // HEAD
    scale = HEAD ** (-0.5)
    shape_q = (batch, tokens_per, heads, HEAD)
    shape_c = (batch, cache_keys.shape[1], heads, HEAD)
    query_four = queries.reshape(shape_q)
    cache_scores = (
        jnp.einsum(
            "bthe,blhe->bhtl",
            query_four,
            cache_keys.reshape(shape_c),
            preferred_element_type=jnp.float32,
        )
        * scale
    )
    valid = jnp.arange(cache_keys.shape[1], dtype=jnp.int32)[None, :] < lengths[:, None]
    cache_scores = jnp.where(valid[:, None, None, :], cache_scores, -jnp.inf)
    draft_scores = (
        jnp.einsum(
            "bthe,bshe->bhts",
            query_four,
            new_keys.reshape(shape_q),
            preferred_element_type=jnp.float32,
        )
        * scale
    )
    draft_scores = jnp.where(reached[:, None] > 0.5, draft_scores, -jnp.inf)
    highest = jnp.maximum(jnp.max(cache_scores, axis=3), jnp.max(draft_scores, axis=3))
    cache_probs = jnp.exp(cache_scores - highest[..., None])
    draft_probs = jnp.exp(draft_scores - highest[..., None])
    totals = jnp.sum(cache_probs, axis=3) + jnp.sum(draft_probs, axis=3)
    mixed = jnp.einsum(
        "bhtl,blhe->bthe",
        cache_probs.astype(jnp.bfloat16),
        cache_values.reshape(shape_c),
        preferred_element_type=jnp.float32,
    )
    mixed = mixed + jnp.einsum(
        "bhts,bshe->bthe",
        draft_probs.astype(jnp.bfloat16),
        new_values.reshape(shape_q),
        preferred_element_type=jnp.float32,
    )
    mixed = mixed / jnp.transpose(totals, (0, 2, 1))[..., None]
    return mixed.reshape(batch, tokens_per, width).astype(jnp.bfloat16)


def expert_rows(rows, expert_gate, expert_up, expert_down):
    gate_part = jnp.dot(rows, expert_gate, preferred_element_type=jnp.float32)
    up_part = jnp.dot(rows, expert_up, preferred_element_type=jnp.float32)
    activation = (jax.nn.silu(gate_part) * up_part).astype(jnp.bfloat16)
    return jnp.dot(activation, expert_down, preferred_element_type=jnp.float32).astype(jnp.bfloat16)


def ring_sum(blocks, shifts):
    total = blocks[0].astype(jnp.float32)
    for step, pairs in enumerate(shifts, start=1):
        total = total + lax.ppermute(blocks[step], "exp", pairs).astype(jnp.float32)
    return total


def ring_reduce_scatter(attended, out_weight, n_exp):
    side = 4
    assert n_exp == side * side
    index = lax.axis_index("exp")
    z_pos, x_pos = index // side, index % side
    cells = [(z, x) for z in range(side) for x in range(side)]
    x_shifts = [[(z * side + x, z * side + (x + k) % side) for z, x in cells] for k in range(1, side)]
    z_shifts = [[(z * side + x, ((z + k) % side) * side + x) for z, x in cells] for k in range(1, side)]
    rows = attended.shape[0] // n_exp
    width = out_weight.shape[1]
    split = width // 2
    blocks = attended.reshape(n_exp, rows, -1)
    near = jnp.arange(side, dtype=jnp.int32)
    z_of = (z_pos + near) % side
    x_of = (x_pos + near) % side
    x_major = (x_of[:, None] + z_of[None, :] * side).reshape(-1)
    z_major = (z_of[:, None] * side + x_of[None, :]).reshape(-1)
    first = jnp.take(blocks, x_major, axis=0).reshape(n_exp * rows, -1)
    first = jnp.dot(first, out_weight[:, :split], preferred_element_type=jnp.float32)
    first = first.astype(jnp.bfloat16).reshape(side, side * rows, split)
    second = jnp.take(blocks, z_major, axis=0).reshape(n_exp * rows, -1)
    second = jnp.dot(second, out_weight[:, split:], preferred_element_type=jnp.float32)
    second = second.astype(jnp.bfloat16).reshape(side, side * rows, split)
    first = ring_sum(first, x_shifts)
    second = ring_sum(second, z_shifts)
    first = ring_sum(first.astype(jnp.bfloat16).reshape(side, rows, split), z_shifts)
    second = ring_sum(second.astype(jnp.bfloat16).reshape(side, rows, split), x_shifts)
    return jnp.concatenate([first, second], axis=1)


def per_device(
    queries,
    new_keys,
    new_values,
    long_keys,
    long_values,
    long_lengths,
    short_keys,
    short_values,
    short_lengths,
    parents,
    accepted,
    residual,
    out_weight,
    norm_gain,
    routes,
    route_weights,
    expert_gate,
    expert_up,
    expert_down,
):
    reached = ancestors(parents)
    head_width = new_keys.shape[2]
    stacked = jnp.concatenate([new_keys, new_values], axis=2)
    compacted = compact_path(reached, accepted, stacked)
    accepted_keys = compacted[:, :, :head_width]
    accepted_values = compacted[:, :, head_width:]
    long_out = attend(
        queries[:1], long_keys, long_values, long_lengths, new_keys[:1], new_values[:1], reached[:1]
    )
    short_out = attend(
        queries[1:],
        short_keys,
        short_values,
        short_lengths,
        new_keys[1:],
        new_values[1:],
        reached[1:],
    )
    attended = jnp.concatenate([long_out, short_out], axis=0).reshape(-1, head_width)
    n_exp = lax.axis_size("exp")
    model_width = out_weight.shape[1]
    attn_proj = ring_reduce_scatter(attended, out_weight, n_exp)
    middle = residual + attn_proj
    normed = (
        middle * lax.rsqrt(jnp.mean(middle * middle, axis=1, keepdims=True) + 1e-05) * norm_gain
    ).astype(jnp.bfloat16)
    tok_rows, top_count = routes.shape
    devices = lax.axis_size("req") * lax.axis_size("exp")
    pieces = max(1, devices // EXPERTS)
    capacity = 2 * tok_rows * top_count // EXPERTS
    flat_routes = routes.reshape(-1)
    flat_count = flat_routes.shape[0]
    expert_ids = jnp.arange(EXPERTS, dtype=jnp.int32)
    onehot = (flat_routes[:, None] == expert_ids[None, :]).astype(jnp.float32)
    flat_ids = jnp.arange(flat_count, dtype=jnp.int32)
    earlier = (flat_ids[:, None] > flat_ids[None, :]).astype(jnp.float32)
    before = jnp.dot(earlier, onehot, precision=lax.Precision.HIGHEST)
    slot_index = jnp.sum(before * onehot, axis=1).astype(jnp.int32).reshape(tok_rows, top_count)
    target = routes * capacity + slot_index
    columns = jnp.arange(EXPERTS * pieces * capacity, dtype=jnp.int32)
    column_target = (columns // (pieces * capacity)) * capacity + columns % capacity
    hits = target[:, :, None] == column_target[None, None, :]
    placement = jnp.any(hits, axis=1).astype(jnp.bfloat16)
    packed = jnp.einsum("tc,td->cd", placement, normed, preferred_element_type=jnp.float32).astype(
        jnp.bfloat16
    )
    outgoing = packed.reshape(devices, capacity, model_width)
    received = lax.all_to_all(outgoing, ("req", "exp"), split_axis=0, concat_axis=0, tiled=True)
    produced = expert_rows(
        received.reshape(-1, model_width), expert_gate[0], expert_up[0], expert_down[0]
    ).reshape(devices, capacity, model_width)
    returned = lax.all_to_all(produced, ("req", "exp"), split_axis=0, concat_axis=0, tiled=True)
    weighing = jnp.sum(jnp.where(hits, route_weights[:, :, None], 0.0), axis=1)
    terms = []
    for _ in range(3):
        term = weighing.astype(jnp.bfloat16)
        terms.append(term)
        weighing = weighing - term.astype(jnp.float32)
    terms = jnp.concatenate(terms, axis=0)
    moe = jnp.dot(terms, returned.reshape(-1, model_width), preferred_element_type=jnp.float32)
    moe = jnp.sum(moe.reshape(3, tok_rows, model_width), axis=0)
    hidden_out = (middle + moe).astype(jnp.bfloat16)
    return (hidden_out, accepted_keys, accepted_values)


def solution(mesh):
    in_specs = (
        P("req", None, "exp"),
        P("req", None, "exp"),
        P("req", None, "exp"),
        P("req", None, "exp"),
        P("req", None, "exp"),
        P("req"),
        P("req", None, "exp"),
        P("req", None, "exp"),
        P("req"),
        P("req", None),
        P("req"),
        P(("req", "exp"), None),
        P("exp", None),
        P(),
        P(("req", "exp"), None),
        P(("req", "exp"), None),
        P(("req", "exp"), None, None),
        P(("req", "exp"), None, None),
        P(("req", "exp"), None, None),
    )
    out_specs = (P(("req", "exp"), None), P("req", None, "exp"), P("req", None, "exp"))
    return jax.shard_map(
        per_device, mesh=mesh, in_specs=in_specs, out_specs=out_specs, check_vma=False
    )
```

```python
import jax
import jax.numpy as jnp
from jax import lax
from jax.sharding import PartitionSpec as P

HEAD = 128
EXPERTS = 64


def ancestors(parents):
    tokens_per = parents.shape[1]
    position = jnp.arange(tokens_per, dtype=jnp.int32)
    identity = (position[:, None] == position[None, :]).astype(jnp.float32)
    linked = (parents[:, :, None] == position[None, None, :]) & (position[None, :, None] > 0)
    reached = jnp.maximum(identity[None], linked.astype(jnp.float32))
    for rounds in range(tokens_per.bit_length()):
        squared = reached.astype(jnp.bfloat16)
        reached = jnp.minimum(
            jnp.einsum("bij,bjk->bik", squared, squared, preferred_element_type=jnp.float32), 1.0
        )
    return reached


def compact_path(reached, accepted, stacked):
    tokens_per = reached.shape[1]
    position = jnp.arange(tokens_per, dtype=jnp.int32)
    levels = jnp.sum(reached, axis=2) - 1.0
    leaf_row = (accepted[:, None] == position[None, :]).astype(jnp.float32)
    on_path = jnp.einsum(
        "bi,bij->bj",
        leaf_row.astype(jnp.bfloat16),
        reached.astype(jnp.bfloat16),
        preferred_element_type=jnp.float32,
    )
    chooser = on_path[:, None, :] * (
        levels[:, None, :] == position[None, :, None].astype(jnp.float32)
    ).astype(jnp.float32)
    return jnp.einsum(
        "btj,bjc->btc", chooser.astype(jnp.bfloat16), stacked, preferred_element_type=jnp.float32
    ).astype(jnp.bfloat16)


def attend(queries, cache_keys, cache_values, lengths, new_keys, new_values, reached):
    batch, tokens_per, width = queries.shape
    heads = width // HEAD
    scale = HEAD ** (-0.5)
    shape_q = (batch, tokens_per, heads, HEAD)
    shape_c = (batch, cache_keys.shape[1], heads, HEAD)
    query_four = queries.reshape(shape_q)
    cache_scores = (
        jnp.einsum(
            "bthe,blhe->bhtl",
            query_four,
            cache_keys.reshape(shape_c),
            preferred_element_type=jnp.float32,
        )
        * scale
    )
    valid = jnp.arange(cache_keys.shape[1], dtype=jnp.int32)[None, :] < lengths[:, None]
    cache_scores = jnp.where(valid[:, None, None, :], cache_scores, -jnp.inf)
    draft_scores = (
        jnp.einsum(
            "bthe,bshe->bhts",
            query_four,
            new_keys.reshape(shape_q),
            preferred_element_type=jnp.float32,
        )
        * scale
    )
    draft_scores = jnp.where(reached[:, None] > 0.5, draft_scores, -jnp.inf)
    highest = jnp.maximum(jnp.max(cache_scores, axis=3), jnp.max(draft_scores, axis=3))
    cache_probs = jnp.exp(cache_scores - highest[..., None])
    draft_probs = jnp.exp(draft_scores - highest[..., None])
    totals = jnp.sum(cache_probs, axis=3) + jnp.sum(draft_probs, axis=3)
    mixed = jnp.einsum(
        "bhtl,blhe->bthe",
        cache_probs.astype(jnp.bfloat16),
        cache_values.reshape(shape_c),
        preferred_element_type=jnp.float32,
    )
    mixed = mixed + jnp.einsum(
        "bhts,bshe->bthe",
        draft_probs.astype(jnp.bfloat16),
        new_values.reshape(shape_q),
        preferred_element_type=jnp.float32,
    )
    mixed = mixed / jnp.transpose(totals, (0, 2, 1))[..., None]
    return mixed.reshape(batch, tokens_per, width).astype(jnp.bfloat16)


def expert_rows(rows, expert_gate, expert_up, expert_down):
    gate_part = jnp.dot(rows, expert_gate, preferred_element_type=jnp.float32)
    up_part = jnp.dot(rows, expert_up, preferred_element_type=jnp.float32)
    activation = (jax.nn.silu(gate_part) * up_part).astype(jnp.bfloat16)
    return jnp.dot(activation, expert_down, preferred_element_type=jnp.float32).astype(jnp.bfloat16)


def ring_gather(shard, shifts):
    parts = [shard] + [lax.ppermute(shard, "exp", pairs) for pairs in shifts]
    return jnp.stack(parts, axis=0)


def gathered_projection(attended, out_weight, n_exp):
    side = 4
    assert n_exp == side * side
    index = lax.axis_index("exp")
    z_pos, x_pos = index // side, index % side
    cells = [(z, x) for z in range(side) for x in range(side)]
    x_shifts = [[(z * side + x, z * side + (x - k) % side) for z, x in cells] for k in range(1, side)]
    z_shifts = [[(z * side + x, ((z - k) % side) * side + x) for z, x in cells] for k in range(1, side)]
    n_req = lax.axis_size("req")
    sibling = [(i, i ^ 1) for i in range(n_req)]
    core = lax.axis_index("req") % 2
    width = out_weight.shape[1]
    half = width // 2
    quarter = half // 2
    mine = lax.dynamic_slice_in_dim(out_weight, core * half, half, axis=1)
    weight_a = ring_gather(ring_gather(mine[:, :quarter], x_shifts), z_shifts)
    weight_b = ring_gather(ring_gather(mine[:, quarter:], z_shifts), x_shifts)
    weight_a = weight_a.reshape(-1, quarter)
    weight_b = weight_b.reshape(-1, quarter)
    rows = attended.shape[0] // n_exp
    heads = lax.all_to_all(
        attended.reshape(n_exp, rows, -1), "exp", split_axis=0, concat_axis=0, tiled=True
    )
    near = jnp.arange(side, dtype=jnp.int32)
    z_of = (z_pos + near) % side
    x_of = (x_pos + near) % side
    z_major = (z_of[:, None] * side + x_of[None, :]).reshape(-1)
    x_major = (x_of[:, None] + z_of[None, :] * side).reshape(-1)
    own_a = jnp.swapaxes(jnp.take(heads, z_major, axis=0), 0, 1).reshape(rows, -1)
    own_b = jnp.swapaxes(jnp.take(heads, x_major, axis=0), 0, 1).reshape(rows, -1)
    own = jnp.stack([own_a, own_b], axis=0)
    other = lax.ppermute(own, "req", sibling)

    def project(pair):
        left = jnp.dot(pair[0], weight_a, preferred_element_type=jnp.float32)
        right = jnp.dot(pair[1], weight_b, preferred_element_type=jnp.float32)
        return jnp.concatenate([left, right], axis=1)

    kept = project(own)
    returned = lax.ppermute(project(other), "req", sibling)
    low = jnp.where(core == 0, kept, returned)
    high = jnp.where(core == 0, returned, kept)
    return jnp.concatenate([low, high], axis=1)


def per_device(
    queries,
    new_keys,
    new_values,
    long_keys,
    long_values,
    long_lengths,
    short_keys,
    short_values,
    short_lengths,
    parents,
    accepted,
    residual,
    out_weight,
    norm_gain,
    routes,
    route_weights,
    expert_gate,
    expert_up,
    expert_down,
):
    reached = ancestors(parents)
    head_width = new_keys.shape[2]
    stacked = jnp.concatenate([new_keys, new_values], axis=2)
    compacted = compact_path(reached, accepted, stacked)
    accepted_keys = compacted[:, :, :head_width]
    accepted_values = compacted[:, :, head_width:]
    long_out = attend(
        queries[:1], long_keys, long_values, long_lengths, new_keys[:1], new_values[:1], reached[:1]
    )
    short_out = attend(
        queries[1:],
        short_keys,
        short_values,
        short_lengths,
        new_keys[1:],
        new_values[1:],
        reached[1:],
    )
    attended = jnp.concatenate([long_out, short_out], axis=0).reshape(-1, head_width)
    n_exp = lax.axis_size("exp")
    model_width = out_weight.shape[1]
    attn_proj = gathered_projection(attended, out_weight, n_exp)
    middle = residual + attn_proj
    normed = (
        middle * lax.rsqrt(jnp.mean(middle * middle, axis=1, keepdims=True) + 1e-05) * norm_gain
    ).astype(jnp.bfloat16)
    tok_rows, top_count = routes.shape
    devices = lax.axis_size("req") * lax.axis_size("exp")
    pieces = max(1, devices // EXPERTS)
    capacity = 2 * tok_rows * top_count // EXPERTS
    flat_routes = routes.reshape(-1)
    flat_count = flat_routes.shape[0]
    expert_ids = jnp.arange(EXPERTS, dtype=jnp.int32)
    onehot = (flat_routes[:, None] == expert_ids[None, :]).astype(jnp.float32)
    flat_ids = jnp.arange(flat_count, dtype=jnp.int32)
    earlier = (flat_ids[:, None] > flat_ids[None, :]).astype(jnp.float32)
    before = jnp.dot(earlier, onehot, precision=lax.Precision.HIGHEST)
    slot_index = jnp.sum(before * onehot, axis=1).astype(jnp.int32).reshape(tok_rows, top_count)
    target = routes * capacity + slot_index
    columns = jnp.arange(EXPERTS * pieces * capacity, dtype=jnp.int32)
    column_target = (columns // (pieces * capacity)) * capacity + columns % capacity
    hits = target[:, :, None] == column_target[None, None, :]
    placement = jnp.any(hits, axis=1).astype(jnp.bfloat16)
    packed = jnp.einsum("tc,td->cd", placement, normed, preferred_element_type=jnp.float32).astype(
        jnp.bfloat16
    )
    outgoing = packed.reshape(devices, capacity, model_width)
    received = lax.all_to_all(outgoing, ("req", "exp"), split_axis=0, concat_axis=0, tiled=True)
    produced = expert_rows(
        received.reshape(-1, model_width), expert_gate[0], expert_up[0], expert_down[0]
    ).reshape(devices, capacity, model_width)
    returned = lax.all_to_all(produced, ("req", "exp"), split_axis=0, concat_axis=0, tiled=True)
    weighing = jnp.sum(jnp.where(hits, route_weights[:, :, None], 0.0), axis=1)
    terms = []
    for _ in range(3):
        term = weighing.astype(jnp.bfloat16)
        terms.append(term)
        weighing = weighing - term.astype(jnp.float32)
    terms = jnp.concatenate(terms, axis=0)
    moe = jnp.dot(terms, returned.reshape(-1, model_width), preferred_element_type=jnp.float32)
    moe = jnp.sum(moe.reshape(3, tok_rows, model_width), axis=0)
    hidden_out = (middle + moe).astype(jnp.bfloat16)
    return (hidden_out, accepted_keys, accepted_values)


def solution(mesh):
    in_specs = (
        P("req", None, "exp"),
        P("req", None, "exp"),
        P("req", None, "exp"),
        P("req", None, "exp"),
        P("req", None, "exp"),
        P("req"),
        P("req", None, "exp"),
        P("req", None, "exp"),
        P("req"),
        P("req", None),
        P("req"),
        P(("req", "exp"), None),
        P("exp", None),
        P(),
        P(("req", "exp"), None),
        P(("req", "exp"), None),
        P(("req", "exp"), None, None),
        P(("req", "exp"), None, None),
        P(("req", "exp"), None, None),
    )
    out_specs = (P(("req", "exp"), None), P("req", None, "exp"), P("req", None, "exp"))
    return jax.shard_map(
        per_device, mesh=mesh, in_specs=in_specs, out_specs=out_specs, check_vma=False
    )
```

```python
import jax
import jax.numpy as jnp
from jax import lax
from jax.sharding import PartitionSpec as P

HEAD = 128
EXPERTS = 64


def ancestors(parents):
    tokens_per = parents.shape[1]
    position = jnp.arange(tokens_per, dtype=jnp.int32)
    identity = (position[:, None] == position[None, :]).astype(jnp.float32)
    linked = (parents[:, :, None] == position[None, None, :]) & (position[None, :, None] > 0)
    reached = jnp.maximum(identity[None], linked.astype(jnp.float32))
    for rounds in range(tokens_per.bit_length()):
        squared = reached.astype(jnp.bfloat16)
        reached = jnp.minimum(
            jnp.einsum("bij,bjk->bik", squared, squared, preferred_element_type=jnp.float32), 1.0
        )
    return reached


def compact_path(reached, accepted, stacked):
    tokens_per = reached.shape[1]
    position = jnp.arange(tokens_per, dtype=jnp.int32)
    levels = jnp.sum(reached, axis=2) - 1.0
    leaf_row = (accepted[:, None] == position[None, :]).astype(jnp.float32)
    on_path = jnp.einsum(
        "bi,bij->bj",
        leaf_row.astype(jnp.bfloat16),
        reached.astype(jnp.bfloat16),
        preferred_element_type=jnp.float32,
    )
    chooser = on_path[:, None, :] * (
        levels[:, None, :] == position[None, :, None].astype(jnp.float32)
    ).astype(jnp.float32)
    return jnp.einsum(
        "btj,bjc->btc", chooser.astype(jnp.bfloat16), stacked, preferred_element_type=jnp.float32
    ).astype(jnp.bfloat16)


def attend(queries, cache_keys, cache_values, lengths, new_keys, new_values, reached):
    batch, tokens_per, width = queries.shape
    heads = width // HEAD
    scale = HEAD ** (-0.5)
    shape_q = (batch, tokens_per, heads, HEAD)
    shape_c = (batch, cache_keys.shape[1], heads, HEAD)
    query_four = queries.reshape(shape_q)
    cache_scores = (
        jnp.einsum(
            "bthe,blhe->bhtl",
            query_four,
            cache_keys.reshape(shape_c),
            preferred_element_type=jnp.float32,
        )
        * scale
    )
    valid = jnp.arange(cache_keys.shape[1], dtype=jnp.int32)[None, :] < lengths[:, None]
    cache_scores = jnp.where(valid[:, None, None, :], cache_scores, -jnp.inf)
    draft_scores = (
        jnp.einsum(
            "bthe,bshe->bhts",
            query_four,
            new_keys.reshape(shape_q),
            preferred_element_type=jnp.float32,
        )
        * scale
    )
    draft_scores = jnp.where(reached[:, None] > 0.5, draft_scores, -jnp.inf)
    highest = jnp.maximum(jnp.max(cache_scores, axis=3), jnp.max(draft_scores, axis=3))
    cache_probs = jnp.exp(cache_scores - highest[..., None])
    draft_probs = jnp.exp(draft_scores - highest[..., None])
    totals = jnp.sum(cache_probs, axis=3) + jnp.sum(draft_probs, axis=3)
    mixed = jnp.einsum(
        "bhtl,blhe->bthe",
        cache_probs.astype(jnp.bfloat16),
        cache_values.reshape(shape_c),
        preferred_element_type=jnp.float32,
    )
    mixed = mixed + jnp.einsum(
        "bhts,bshe->bthe",
        draft_probs.astype(jnp.bfloat16),
        new_values.reshape(shape_q),
        preferred_element_type=jnp.float32,
    )
    mixed = mixed / jnp.transpose(totals, (0, 2, 1))[..., None]
    return mixed.reshape(batch, tokens_per, width).astype(jnp.bfloat16)


def expert_rows(rows, expert_gate, expert_up, expert_down):
    gate_part = jnp.dot(rows, expert_gate, preferred_element_type=jnp.float32)
    up_part = jnp.dot(rows, expert_up, preferred_element_type=jnp.float32)
    activation = (jax.nn.silu(gate_part) * up_part).astype(jnp.bfloat16)
    return jnp.dot(activation, expert_down, preferred_element_type=jnp.float32).astype(jnp.bfloat16)


def ring_sum(blocks, shifts):
    total = blocks[0].astype(jnp.float32)
    for step, pairs in enumerate(shifts, start=1):
        total = total + lax.ppermute(blocks[step], "exp", pairs).astype(jnp.float32)
    return total


def ring_reduce_scatter(attended, out_weight, n_exp):
    side = 4
    assert n_exp == side * side
    index = lax.axis_index("exp")
    z_pos, x_pos = index // side, index % side
    cells = [(z, x) for z in range(side) for x in range(side)]
    x_shifts = [[(z * side + x, z * side + (x + k) % side) for z, x in cells] for k in range(1, side)]
    z_shifts = [[(z * side + x, ((z + k) % side) * side + x) for z, x in cells] for k in range(1, side)]
    rows = attended.shape[0] // n_exp
    width = out_weight.shape[1]
    split = width // 2
    blocks = attended.reshape(n_exp, rows, -1)
    near = jnp.arange(side, dtype=jnp.int32)
    z_of = (z_pos + near) % side
    x_of = (x_pos + near) % side
    x_major = (x_of[:, None] + z_of[None, :] * side).reshape(-1)
    z_major = (z_of[:, None] * side + x_of[None, :]).reshape(-1)
    first = jnp.take(blocks, x_major, axis=0).reshape(n_exp * rows, -1)
    first = jnp.dot(first, out_weight[:, :split], preferred_element_type=jnp.float32)
    first = first.astype(jnp.bfloat16).reshape(side, side * rows, split)
    second = jnp.take(blocks, z_major, axis=0).reshape(n_exp * rows, -1)
    second = jnp.dot(second, out_weight[:, split:], preferred_element_type=jnp.float32)
    second = second.astype(jnp.bfloat16).reshape(side, side * rows, split)
    first, second = lax.optimization_barrier((first, second))
    first = ring_sum(first, x_shifts)
    second = ring_sum(second, z_shifts)
    first = ring_sum(first.astype(jnp.bfloat16).reshape(side, rows, split), z_shifts)
    second = ring_sum(second.astype(jnp.bfloat16).reshape(side, rows, split), x_shifts)
    return jnp.concatenate([first, second], axis=1)


def per_device(
    queries,
    new_keys,
    new_values,
    long_keys,
    long_values,
    long_lengths,
    short_keys,
    short_values,
    short_lengths,
    parents,
    accepted,
    residual,
    out_weight,
    norm_gain,
    routes,
    route_weights,
    expert_gate,
    expert_up,
    expert_down,
):
    reached = ancestors(parents)
    head_width = new_keys.shape[2]
    stacked = jnp.concatenate([new_keys, new_values], axis=2)
    compacted = compact_path(reached, accepted, stacked)
    accepted_keys = compacted[:, :, :head_width]
    accepted_values = compacted[:, :, head_width:]
    long_out = attend(
        queries[:1], long_keys, long_values, long_lengths, new_keys[:1], new_values[:1], reached[:1]
    )
    short_out = attend(
        queries[1:],
        short_keys,
        short_values,
        short_lengths,
        new_keys[1:],
        new_values[1:],
        reached[1:],
    )
    attended = jnp.concatenate([long_out, short_out], axis=0).reshape(-1, head_width)
    n_exp = lax.axis_size("exp")
    model_width = out_weight.shape[1]
    attn_proj = ring_reduce_scatter(attended, out_weight, n_exp)
    middle = residual + attn_proj
    normed = (
        middle * lax.rsqrt(jnp.mean(middle * middle, axis=1, keepdims=True) + 1e-05) * norm_gain
    ).astype(jnp.bfloat16)
    tok_rows, top_count = routes.shape
    devices = lax.axis_size("req") * lax.axis_size("exp")
    pieces = max(1, devices // EXPERTS)
    capacity = 2 * tok_rows * top_count // EXPERTS
    flat_routes = routes.reshape(-1)
    flat_count = flat_routes.shape[0]
    expert_ids = jnp.arange(EXPERTS, dtype=jnp.int32)
    onehot = (flat_routes[:, None] == expert_ids[None, :]).astype(jnp.float32)
    flat_ids = jnp.arange(flat_count, dtype=jnp.int32)
    earlier = (flat_ids[:, None] > flat_ids[None, :]).astype(jnp.float32)
    before = jnp.dot(earlier, onehot, precision=lax.Precision.HIGHEST)
    slot_index = jnp.sum(before * onehot, axis=1).astype(jnp.int32).reshape(tok_rows, top_count)
    target = routes * capacity + slot_index
    columns = jnp.arange(EXPERTS * pieces * capacity, dtype=jnp.int32)
    column_target = (columns // (pieces * capacity)) * capacity + columns % capacity
    hits = target[:, :, None] == column_target[None, None, :]
    placement = jnp.any(hits, axis=1).astype(jnp.bfloat16)
    packed = jnp.einsum("tc,td->cd", placement, normed, preferred_element_type=jnp.float32).astype(
        jnp.bfloat16
    )
    outgoing = packed.reshape(devices, capacity, model_width)
    received = lax.all_to_all(outgoing, ("req", "exp"), split_axis=0, concat_axis=0, tiled=True)
    produced = expert_rows(
        received.reshape(-1, model_width), expert_gate[0], expert_up[0], expert_down[0]
    ).reshape(devices, capacity, model_width)
    returned = lax.all_to_all(produced, ("req", "exp"), split_axis=0, concat_axis=0, tiled=True)
    weighing = jnp.sum(jnp.where(hits, route_weights[:, :, None], 0.0), axis=1)
    terms = []
    for _ in range(3):
        term = weighing.astype(jnp.bfloat16)
        terms.append(term)
        weighing = weighing - term.astype(jnp.float32)
    terms = jnp.concatenate(terms, axis=0)
    moe = jnp.dot(terms, returned.reshape(-1, model_width), preferred_element_type=jnp.float32)
    moe = jnp.sum(moe.reshape(3, tok_rows, model_width), axis=0)
    hidden_out = (middle + moe).astype(jnp.bfloat16)
    return (hidden_out, accepted_keys, accepted_values)


def solution(mesh):
    in_specs = (
        P("req", None, "exp"),
        P("req", None, "exp"),
        P("req", None, "exp"),
        P("req", None, "exp"),
        P("req", None, "exp"),
        P("req"),
        P("req", None, "exp"),
        P("req", None, "exp"),
        P("req"),
        P("req", None),
        P("req"),
        P(("req", "exp"), None),
        P("exp", None),
        P(),
        P(("req", "exp"), None),
        P(("req", "exp"), None),
        P(("req", "exp"), None, None),
        P(("req", "exp"), None, None),
        P(("req", "exp"), None, None),
    )
    out_specs = (P(("req", "exp"), None), P("req", None, "exp"), P("req", None, "exp"))
    return jax.shard_map(
        per_device, mesh=mesh, in_specs=in_specs, out_specs=out_specs, check_vma=False
    )
```

```python
import jax
import jax.numpy as jnp
from jax import lax
from jax.sharding import PartitionSpec as P

HEAD = 128
EXPERTS = 64


def ancestors(parents):
    tokens_per = parents.shape[1]
    position = jnp.arange(tokens_per, dtype=jnp.int32)
    identity = (position[:, None] == position[None, :]).astype(jnp.float32)
    linked = (parents[:, :, None] == position[None, None, :]) & (position[None, :, None] > 0)
    reached = jnp.maximum(identity[None], linked.astype(jnp.float32))
    for rounds in range(tokens_per.bit_length()):
        squared = reached.astype(jnp.bfloat16)
        reached = jnp.minimum(
            jnp.einsum("bij,bjk->bik", squared, squared, preferred_element_type=jnp.float32), 1.0
        )
    return reached


def compact_path(reached, accepted, stacked):
    tokens_per = reached.shape[1]
    position = jnp.arange(tokens_per, dtype=jnp.int32)
    levels = jnp.sum(reached, axis=2) - 1.0
    leaf_row = (accepted[:, None] == position[None, :]).astype(jnp.float32)
    on_path = jnp.einsum(
        "bi,bij->bj",
        leaf_row.astype(jnp.bfloat16),
        reached.astype(jnp.bfloat16),
        preferred_element_type=jnp.float32,
    )
    chooser = on_path[:, None, :] * (
        levels[:, None, :] == position[None, :, None].astype(jnp.float32)
    ).astype(jnp.float32)
    return jnp.einsum(
        "btj,bjc->btc", chooser.astype(jnp.bfloat16), stacked, preferred_element_type=jnp.float32
    ).astype(jnp.bfloat16)


def attend(queries, cache_keys, cache_values, lengths, new_keys, new_values, reached):
    batch, tokens_per, width = queries.shape
    heads = width // HEAD
    scale = HEAD ** (-0.5)
    shape_q = (batch, tokens_per, heads, HEAD)
    shape_n = (batch, new_keys.shape[1], heads, HEAD)
    shape_c = (batch, cache_keys.shape[1], heads, HEAD)
    query_four = queries.reshape(shape_q)
    cache_scores = (
        jnp.einsum(
            "bthe,blhe->bhtl",
            query_four,
            cache_keys.reshape(shape_c),
            preferred_element_type=jnp.float32,
        )
        * scale
    )
    valid = jnp.arange(cache_keys.shape[1], dtype=jnp.int32)[None, :] < lengths[:, None]
    cache_scores = jnp.where(valid[:, None, None, :], cache_scores, -jnp.inf)
    draft_scores = (
        jnp.einsum(
            "bthe,bshe->bhts",
            query_four,
            new_keys.reshape(shape_n),
            preferred_element_type=jnp.float32,
        )
        * scale
    )
    draft_scores = jnp.where(reached[:, None] > 0.5, draft_scores, -jnp.inf)
    highest = jnp.maximum(jnp.max(cache_scores, axis=3), jnp.max(draft_scores, axis=3))
    cache_probs = jnp.exp(cache_scores - highest[..., None])
    draft_probs = jnp.exp(draft_scores - highest[..., None])
    totals = jnp.sum(cache_probs, axis=3) + jnp.sum(draft_probs, axis=3)
    mixed = jnp.einsum(
        "bhtl,blhe->bthe",
        cache_probs.astype(jnp.bfloat16),
        cache_values.reshape(shape_c),
        preferred_element_type=jnp.float32,
    )
    mixed = mixed + jnp.einsum(
        "bhts,bshe->bthe",
        draft_probs.astype(jnp.bfloat16),
        new_values.reshape(shape_n),
        preferred_element_type=jnp.float32,
    )
    mixed = mixed / jnp.transpose(totals, (0, 2, 1))[..., None]
    return mixed.reshape(batch, tokens_per, width).astype(jnp.bfloat16)


def expert_rows(rows, expert_gate, expert_up, expert_down):
    gate_part = jnp.dot(rows, expert_gate, preferred_element_type=jnp.float32)
    up_part = jnp.dot(rows, expert_up, preferred_element_type=jnp.float32)
    activation = (jax.nn.silu(gate_part) * up_part).astype(jnp.bfloat16)
    return jnp.dot(activation, expert_down, preferred_element_type=jnp.float32).astype(jnp.bfloat16)


def ring_sum(blocks, shifts):
    total = blocks[0].astype(jnp.float32)
    for step, pairs in enumerate(shifts, start=1):
        total = total + lax.ppermute(blocks[step], "exp", pairs).astype(jnp.float32)
    return total


def half_reduce_scatter(attended, out_weight, n_exp, x_first):
    side = 4
    assert n_exp == side * side
    index = lax.axis_index("exp")
    z_pos, x_pos = index // side, index % side
    cells = [(z, x) for z in range(side) for x in range(side)]
    x_shifts = [[(z * side + x, z * side + (x + k) % side) for z, x in cells] for k in range(1, side)]
    z_shifts = [[(z * side + x, ((z + k) % side) * side + x) for z, x in cells] for k in range(1, side)]
    rows = attended.shape[0] // n_exp
    width = out_weight.shape[1]
    blocks = attended.reshape(n_exp, rows, -1)
    near = jnp.arange(side, dtype=jnp.int32)
    z_of = (z_pos + near) % side
    x_of = (x_pos + near) % side
    if x_first:
        order = (x_of[:, None] + z_of[None, :] * side).reshape(-1)
        first_shifts, second_shifts = x_shifts, z_shifts
    else:
        order = (z_of[:, None] * side + x_of[None, :]).reshape(-1)
        first_shifts, second_shifts = z_shifts, x_shifts
    part = jnp.take(blocks, order, axis=0).reshape(n_exp * rows, -1)
    part = jnp.dot(part, out_weight, preferred_element_type=jnp.float32)
    part = ring_sum(part.astype(jnp.bfloat16).reshape(side, side * rows, width), first_shifts)
    return ring_sum(part.astype(jnp.bfloat16).reshape(side, rows, width), second_shifts)


def per_device(
    queries,
    new_keys,
    new_values,
    long_keys,
    long_values,
    long_lengths,
    short_keys,
    short_values,
    short_lengths,
    parents,
    accepted,
    residual,
    out_weight,
    norm_gain,
    routes,
    route_weights,
    expert_gate,
    expert_up,
    expert_down,
):
    reached = ancestors(parents)
    head_width = new_keys.shape[2]
    stacked = jnp.concatenate([new_keys, new_values], axis=2)
    compacted = compact_path(reached, accepted, stacked)
    accepted_keys = compacted[:, :, :head_width]
    accepted_values = compacted[:, :, head_width:]
    n_exp = lax.axis_size("exp")
    halves = 2
    q_rows = queries.shape[1] // halves
    reduced = []
    for half in range(halves):
        rows = slice(half * q_rows, (half + 1) * q_rows)
        long_out = attend(
            queries[:1, rows],
            long_keys,
            long_values,
            long_lengths,
            new_keys[:1],
            new_values[:1],
            reached[:1, rows],
        )
        short_out = attend(
            queries[1:, rows],
            short_keys,
            short_values,
            short_lengths,
            new_keys[1:],
            new_values[1:],
            reached[1:, rows],
        )
        attended = jnp.concatenate([long_out, short_out], axis=0).reshape(-1, head_width)
        reduced.append(half_reduce_scatter(attended, out_weight, n_exp, half == 0))
    attn_proj = jnp.concatenate(reduced, axis=0)
    model_width = out_weight.shape[1]
    middle = residual + attn_proj
    normed = (
        middle * lax.rsqrt(jnp.mean(middle * middle, axis=1, keepdims=True) + 1e-05) * norm_gain
    ).astype(jnp.bfloat16)
    tok_rows, top_count = routes.shape
    devices = lax.axis_size("req") * lax.axis_size("exp")
    pieces = max(1, devices // EXPERTS)
    capacity = 2 * tok_rows * top_count // EXPERTS
    flat_routes = routes.reshape(-1)
    flat_count = flat_routes.shape[0]
    expert_ids = jnp.arange(EXPERTS, dtype=jnp.int32)
    onehot = (flat_routes[:, None] == expert_ids[None, :]).astype(jnp.float32)
    flat_ids = jnp.arange(flat_count, dtype=jnp.int32)
    earlier = (flat_ids[:, None] > flat_ids[None, :]).astype(jnp.float32)
    before = jnp.dot(earlier, onehot, precision=lax.Precision.HIGHEST)
    slot_index = jnp.sum(before * onehot, axis=1).astype(jnp.int32).reshape(tok_rows, top_count)
    target = routes * capacity + slot_index
    columns = jnp.arange(EXPERTS * pieces * capacity, dtype=jnp.int32)
    column_target = (columns // (pieces * capacity)) * capacity + columns % capacity
    hits = target[:, :, None] == column_target[None, None, :]
    placement = jnp.any(hits, axis=1).astype(jnp.bfloat16)
    packed = jnp.einsum("tc,td->cd", placement, normed, preferred_element_type=jnp.float32).astype(
        jnp.bfloat16
    )
    outgoing = packed.reshape(devices, capacity, model_width)
    received = lax.all_to_all(outgoing, ("req", "exp"), split_axis=0, concat_axis=0, tiled=True)
    produced = expert_rows(
        received.reshape(-1, model_width), expert_gate[0], expert_up[0], expert_down[0]
    ).reshape(devices, capacity, model_width)
    returned = lax.all_to_all(produced, ("req", "exp"), split_axis=0, concat_axis=0, tiled=True)
    weighing = jnp.sum(jnp.where(hits, route_weights[:, :, None], 0.0), axis=1)
    terms = []
    for _ in range(3):
        term = weighing.astype(jnp.bfloat16)
        terms.append(term)
        weighing = weighing - term.astype(jnp.float32)
    terms = jnp.concatenate(terms, axis=0)
    moe = jnp.dot(terms, returned.reshape(-1, model_width), preferred_element_type=jnp.float32)
    moe = jnp.sum(moe.reshape(3, tok_rows, model_width), axis=0)
    hidden_out = (middle + moe).astype(jnp.bfloat16)
    return (hidden_out, accepted_keys, accepted_values)


def solution(mesh):
    in_specs = (
        P("req", None, "exp"),
        P("req", None, "exp"),
        P("req", None, "exp"),
        P("req", None, "exp"),
        P("req", None, "exp"),
        P("req"),
        P("req", None, "exp"),
        P("req", None, "exp"),
        P("req"),
        P("req", None),
        P("req"),
        P(("req", "exp"), None),
        P("exp", None),
        P(),
        P(("req", "exp"), None),
        P(("req", "exp"), None),
        P(("req", "exp"), None, None),
        P(("req", "exp"), None, None),
        P(("req", "exp"), None, None),
    )
    out_specs = (P(("req", "exp"), None), P("req", None, "exp"), P("req", None, "exp"))
    return jax.shard_map(
        per_device, mesh=mesh, in_specs=in_specs, out_specs=out_specs, check_vma=False
    )
```

```python
import jax
import jax.numpy as jnp
from jax import lax
from jax.sharding import PartitionSpec as P

HEAD = 128
EXPERTS = 64


def ancestors(parents):
    tokens_per = parents.shape[1]
    position = jnp.arange(tokens_per, dtype=jnp.int32)
    identity = (position[:, None] == position[None, :]).astype(jnp.float32)
    linked = (parents[:, :, None] == position[None, None, :]) & (position[None, :, None] > 0)
    reached = jnp.maximum(identity[None], linked.astype(jnp.float32))
    for rounds in range(tokens_per.bit_length()):
        squared = reached.astype(jnp.bfloat16)
        reached = jnp.minimum(
            jnp.einsum("bij,bjk->bik", squared, squared, preferred_element_type=jnp.float32), 1.0
        )
    return reached


def compact_path(reached, accepted, stacked):
    tokens_per = reached.shape[1]
    position = jnp.arange(tokens_per, dtype=jnp.int32)
    levels = jnp.sum(reached, axis=2) - 1.0
    leaf_row = (accepted[:, None] == position[None, :]).astype(jnp.float32)
    on_path = jnp.einsum(
        "bi,bij->bj",
        leaf_row.astype(jnp.bfloat16),
        reached.astype(jnp.bfloat16),
        preferred_element_type=jnp.float32,
    )
    chooser = on_path[:, None, :] * (
        levels[:, None, :] == position[None, :, None].astype(jnp.float32)
    ).astype(jnp.float32)
    return jnp.einsum(
        "btj,bjc->btc", chooser.astype(jnp.bfloat16), stacked, preferred_element_type=jnp.float32
    ).astype(jnp.bfloat16)


def attend(queries, cache_keys, cache_values, lengths, new_keys, new_values, reached):
    batch, tokens_per, width = queries.shape
    heads = width // HEAD
    scale = HEAD ** (-0.5)
    shape_q = (batch, tokens_per, heads, HEAD)
    shape_c = (batch, cache_keys.shape[1], heads, HEAD)
    query_four = queries.reshape(shape_q)
    cache_scores = (
        jnp.einsum(
            "bthe,blhe->bhtl",
            query_four,
            cache_keys.reshape(shape_c),
            preferred_element_type=jnp.float32,
        )
        * scale
    )
    valid = jnp.arange(cache_keys.shape[1], dtype=jnp.int32)[None, :] < lengths[:, None]
    cache_scores = jnp.where(valid[:, None, None, :], cache_scores, -jnp.inf)
    draft_scores = (
        jnp.einsum(
            "bthe,bshe->bhts",
            query_four,
            new_keys.reshape(shape_q),
            preferred_element_type=jnp.float32,
        )
        * scale
    )
    draft_scores = jnp.where(reached[:, None] > 0.5, draft_scores, -jnp.inf)
    highest = jnp.maximum(jnp.max(cache_scores, axis=3), jnp.max(draft_scores, axis=3))
    cache_probs = jnp.exp(cache_scores - highest[..., None])
    draft_probs = jnp.exp(draft_scores - highest[..., None])
    totals = jnp.sum(cache_probs, axis=3) + jnp.sum(draft_probs, axis=3)
    mixed = jnp.einsum(
        "bhtl,blhe->bthe",
        cache_probs.astype(jnp.bfloat16),
        cache_values.reshape(shape_c),
        preferred_element_type=jnp.float32,
    )
    mixed = mixed + jnp.einsum(
        "bhts,bshe->bthe",
        draft_probs.astype(jnp.bfloat16),
        new_values.reshape(shape_q),
        preferred_element_type=jnp.float32,
    )
    mixed = mixed / jnp.transpose(totals, (0, 2, 1))[..., None]
    return mixed.reshape(batch, tokens_per, width).astype(jnp.bfloat16)


def expert_rows(rows, expert_gate, expert_up, expert_down):
    gate_part = jnp.dot(rows, expert_gate, preferred_element_type=jnp.float32)
    up_part = jnp.dot(rows, expert_up, preferred_element_type=jnp.float32)
    activation = (jax.nn.silu(gate_part) * up_part).astype(jnp.bfloat16)
    return jnp.dot(activation, expert_down, preferred_element_type=jnp.float32).astype(jnp.bfloat16)


def ring_sum(blocks, shifts):
    total = blocks[0].astype(jnp.float32)
    for step in (2, 1, 3):
        total = total + lax.ppermute(blocks[step], "exp", shifts[step - 1]).astype(jnp.float32)
    return total


def ring_reduce_scatter(attended, out_weight, n_exp):
    side = 4
    assert n_exp == side * side
    index = lax.axis_index("exp")
    z_pos, x_pos = index // side, index % side
    cells = [(z, x) for z in range(side) for x in range(side)]
    x_shifts = [[(z * side + x, z * side + (x + k) % side) for z, x in cells] for k in range(1, side)]
    z_shifts = [[(z * side + x, ((z + k) % side) * side + x) for z, x in cells] for k in range(1, side)]
    rows = attended.shape[0] // n_exp
    width = out_weight.shape[1]
    split = width // 2
    blocks = attended.reshape(n_exp, rows, -1)
    near = jnp.arange(side, dtype=jnp.int32)
    z_of = (z_pos + near) % side
    x_of = (x_pos + near) % side
    x_major = (x_of[:, None] + z_of[None, :] * side).reshape(-1)
    z_major = (z_of[:, None] * side + x_of[None, :]).reshape(-1)
    first = jnp.take(blocks, x_major, axis=0).reshape(n_exp * rows, -1)
    first = jnp.dot(first, out_weight[:, :split], preferred_element_type=jnp.float32)
    first = first.astype(jnp.bfloat16).reshape(side, side * rows, split)
    second = jnp.take(blocks, z_major, axis=0).reshape(n_exp * rows, -1)
    second = jnp.dot(second, out_weight[:, split:], preferred_element_type=jnp.float32)
    second = second.astype(jnp.bfloat16).reshape(side, side * rows, split)
    first, second = lax.optimization_barrier((first, second))
    first = ring_sum(first, x_shifts)
    second = ring_sum(second, z_shifts)
    first = ring_sum(first.astype(jnp.bfloat16).reshape(side, rows, split), z_shifts)
    second = ring_sum(second.astype(jnp.bfloat16).reshape(side, rows, split), x_shifts)
    return jnp.concatenate([first, second], axis=1)


def per_device(
    queries,
    new_keys,
    new_values,
    long_keys,
    long_values,
    long_lengths,
    short_keys,
    short_values,
    short_lengths,
    parents,
    accepted,
    residual,
    out_weight,
    norm_gain,
    routes,
    route_weights,
    expert_gate,
    expert_up,
    expert_down,
):
    reached = ancestors(parents)
    head_width = new_keys.shape[2]
    stacked = jnp.concatenate([new_keys, new_values], axis=2)
    compacted = compact_path(reached, accepted, stacked)
    accepted_keys = compacted[:, :, :head_width]
    accepted_values = compacted[:, :, head_width:]
    long_out = attend(
        queries[:1], long_keys, long_values, long_lengths, new_keys[:1], new_values[:1], reached[:1]
    )
    short_out = attend(
        queries[1:],
        short_keys,
        short_values,
        short_lengths,
        new_keys[1:],
        new_values[1:],
        reached[1:],
    )
    attended = jnp.concatenate([long_out, short_out], axis=0).reshape(-1, head_width)
    n_exp = lax.axis_size("exp")
    model_width = out_weight.shape[1]
    attn_proj = ring_reduce_scatter(attended, out_weight, n_exp)
    middle = residual + attn_proj
    normed = (
        middle * lax.rsqrt(jnp.mean(middle * middle, axis=1, keepdims=True) + 1e-05) * norm_gain
    ).astype(jnp.bfloat16)
    tok_rows, top_count = routes.shape
    devices = lax.axis_size("req") * lax.axis_size("exp")
    pieces = max(1, devices // EXPERTS)
    capacity = 2 * tok_rows * top_count // EXPERTS
    flat_routes = routes.reshape(-1)
    flat_count = flat_routes.shape[0]
    expert_ids = jnp.arange(EXPERTS, dtype=jnp.int32)
    onehot = (flat_routes[:, None] == expert_ids[None, :]).astype(jnp.float32)
    flat_ids = jnp.arange(flat_count, dtype=jnp.int32)
    earlier = (flat_ids[:, None] > flat_ids[None, :]).astype(jnp.float32)
    before = jnp.dot(earlier, onehot, precision=lax.Precision.HIGHEST)
    slot_index = jnp.sum(before * onehot, axis=1).astype(jnp.int32).reshape(tok_rows, top_count)
    target = routes * capacity + slot_index
    columns = jnp.arange(EXPERTS * pieces * capacity, dtype=jnp.int32)
    column_target = (columns // (pieces * capacity)) * capacity + columns % capacity
    hits = target[:, :, None] == column_target[None, None, :]
    placement = jnp.any(hits, axis=1).astype(jnp.bfloat16)
    packed = jnp.einsum("tc,td->cd", placement, normed, preferred_element_type=jnp.float32).astype(
        jnp.bfloat16
    )
    outgoing = packed.reshape(devices, capacity, model_width)
    received = lax.all_to_all(outgoing, ("req", "exp"), split_axis=0, concat_axis=0, tiled=True)
    produced = expert_rows(
        received.reshape(-1, model_width), expert_gate[0], expert_up[0], expert_down[0]
    ).reshape(devices, capacity, model_width)
    returned = lax.all_to_all(produced, ("req", "exp"), split_axis=0, concat_axis=0, tiled=True)
    weighing = jnp.sum(jnp.where(hits, route_weights[:, :, None], 0.0), axis=1)
    terms = []
    for _ in range(3):
        term = weighing.astype(jnp.bfloat16)
        terms.append(term)
        weighing = weighing - term.astype(jnp.float32)
    terms = jnp.concatenate(terms, axis=0)
    moe = jnp.dot(terms, returned.reshape(-1, model_width), preferred_element_type=jnp.float32)
    moe = jnp.sum(moe.reshape(3, tok_rows, model_width), axis=0)
    hidden_out = (middle + moe).astype(jnp.bfloat16)
    return (hidden_out, accepted_keys, accepted_values)


def solution(mesh):
    in_specs = (
        P("req", None, "exp"),
        P("req", None, "exp"),
        P("req", None, "exp"),
        P("req", None, "exp"),
        P("req", None, "exp"),
        P("req"),
        P("req", None, "exp"),
        P("req", None, "exp"),
        P("req"),
        P("req", None),
        P("req"),
        P(("req", "exp"), None),
        P("exp", None),
        P(),
        P(("req", "exp"), None),
        P(("req", "exp"), None),
        P(("req", "exp"), None, None),
        P(("req", "exp"), None, None),
        P(("req", "exp"), None, None),
    )
    out_specs = (P(("req", "exp"), None), P("req", None, "exp"), P("req", None, "exp"))
    return jax.shard_map(
        per_device, mesh=mesh, in_specs=in_specs, out_specs=out_specs, check_vma=False
    )
```

```python
import jax
import jax.numpy as jnp
from jax import lax
from jax.sharding import PartitionSpec as P

HEAD = 128
EXPERTS = 64


def ancestors(parents):
    tokens_per = parents.shape[1]
    position = jnp.arange(tokens_per, dtype=jnp.int32)
    identity = (position[:, None] == position[None, :]).astype(jnp.float32)
    linked = (parents[:, :, None] == position[None, None, :]) & (position[None, :, None] > 0)
    reached = jnp.maximum(identity[None], linked.astype(jnp.float32))
    for rounds in range(tokens_per.bit_length()):
        squared = reached.astype(jnp.bfloat16)
        reached = jnp.minimum(
            jnp.einsum("bij,bjk->bik", squared, squared, preferred_element_type=jnp.float32), 1.0
        )
    return reached


def compact_path(reached, accepted, stacked):
    tokens_per = reached.shape[1]
    position = jnp.arange(tokens_per, dtype=jnp.int32)
    levels = jnp.sum(reached, axis=2) - 1.0
    leaf_row = (accepted[:, None] == position[None, :]).astype(jnp.float32)
    on_path = jnp.einsum(
        "bi,bij->bj",
        leaf_row.astype(jnp.bfloat16),
        reached.astype(jnp.bfloat16),
        preferred_element_type=jnp.float32,
    )
    chooser = on_path[:, None, :] * (
        levels[:, None, :] == position[None, :, None].astype(jnp.float32)
    ).astype(jnp.float32)
    return jnp.einsum(
        "btj,bjc->btc", chooser.astype(jnp.bfloat16), stacked, preferred_element_type=jnp.float32
    ).astype(jnp.bfloat16)


def attend(queries, cache_keys, cache_values, lengths, new_keys, new_values, reached):
    batch, tokens_per, width = queries.shape
    heads = width // HEAD
    scale = HEAD ** (-0.5)
    shape_q = (batch, tokens_per, heads, HEAD)
    shape_c = (batch, cache_keys.shape[1], heads, HEAD)
    query_four = queries.reshape(shape_q)
    cache_scores = (
        jnp.einsum(
            "bthe,blhe->bhtl",
            query_four,
            cache_keys.reshape(shape_c),
            preferred_element_type=jnp.float32,
        )
        * scale
    )
    valid = jnp.arange(cache_keys.shape[1], dtype=jnp.int32)[None, :] < lengths[:, None]
    cache_scores = jnp.where(valid[:, None, None, :], cache_scores, -jnp.inf)
    draft_scores = (
        jnp.einsum(
            "bthe,bshe->bhts",
            query_four,
            new_keys.reshape(shape_q),
            preferred_element_type=jnp.float32,
        )
        * scale
    )
    draft_scores = jnp.where(reached[:, None] > 0.5, draft_scores, -jnp.inf)
    highest = jnp.maximum(jnp.max(cache_scores, axis=3), jnp.max(draft_scores, axis=3))
    cache_probs = jnp.exp(cache_scores - highest[..., None])
    draft_probs = jnp.exp(draft_scores - highest[..., None])
    totals = jnp.sum(cache_probs, axis=3) + jnp.sum(draft_probs, axis=3)
    mixed = jnp.einsum(
        "bhtl,blhe->bthe",
        cache_probs.astype(jnp.bfloat16),
        cache_values.reshape(shape_c),
        preferred_element_type=jnp.float32,
    )
    mixed = mixed + jnp.einsum(
        "bhts,bshe->bthe",
        draft_probs.astype(jnp.bfloat16),
        new_values.reshape(shape_q),
        preferred_element_type=jnp.float32,
    )
    mixed = mixed / jnp.transpose(totals, (0, 2, 1))[..., None]
    return mixed.reshape(batch, tokens_per, width).astype(jnp.bfloat16)


def expert_rows(rows, expert_gate, expert_up, expert_down):
    gate_part = jnp.dot(rows, expert_gate, preferred_element_type=jnp.float32)
    up_part = jnp.dot(rows, expert_up, preferred_element_type=jnp.float32)
    activation = (jax.nn.silu(gate_part) * up_part).astype(jnp.bfloat16)
    return jnp.dot(activation, expert_down, preferred_element_type=jnp.float32).astype(jnp.bfloat16)


def ring_sum(blocks, shifts):
    total = blocks[0].astype(jnp.float32)
    for step, pairs in enumerate(shifts, start=1):
        total = total + lax.ppermute(blocks[step], "exp", pairs).astype(jnp.float32)
    return total


def ring_reduce_scatter(attended, out_weight, n_exp):
    side = 4
    assert n_exp == side * side
    index = lax.axis_index("exp")
    z_pos, x_pos = index // side, index % side
    cells = [(z, x) for z in range(side) for x in range(side)]
    x_shifts = [[(z * side + x, z * side + (x + k) % side) for z, x in cells] for k in range(1, side)]
    z_shifts = [[(z * side + x, ((z + k) % side) * side + x) for z, x in cells] for k in range(1, side)]
    rows = attended.shape[0] // n_exp
    width = out_weight.shape[1]
    split = width // 2
    blocks = attended.reshape(n_exp, rows, -1)
    near = jnp.arange(side, dtype=jnp.int32)
    z_of = (z_pos + near) % side
    x_of = (x_pos + near) % side
    x_major = (x_of[:, None] + z_of[None, :] * side).reshape(-1)
    z_major = (z_of[:, None] * side + x_of[None, :]).reshape(-1)
    first = jnp.take(blocks, x_major, axis=0).reshape(n_exp * rows, -1)
    first = jnp.dot(first, out_weight[:, :split], preferred_element_type=jnp.float32)
    first = first.astype(jnp.bfloat16).reshape(side, side * rows, split)
    second = jnp.take(blocks, z_major, axis=0).reshape(n_exp * rows, -1)
    second = jnp.dot(second, out_weight[:, split:], preferred_element_type=jnp.float32)
    second = second.astype(jnp.bfloat16).reshape(side, side * rows, split)
    first, second = lax.optimization_barrier((first, second))
    first = ring_sum(first, x_shifts)
    second = ring_sum(second, z_shifts)
    first = ring_sum(first.astype(jnp.bfloat16).reshape(side, rows, split), z_shifts)
    second = ring_sum(second.astype(jnp.bfloat16).reshape(side, rows, split), x_shifts)
    return jnp.concatenate([first, second], axis=1)


def slot_of(routes):
    tok_rows, top_count = routes.shape
    flat_routes = routes.reshape(-1)
    flat_count = flat_routes.shape[0]
    expert_ids = jnp.arange(EXPERTS, dtype=jnp.int32)
    onehot = (flat_routes[:, None] == expert_ids[None, :]).astype(jnp.float32)
    flat_ids = jnp.arange(flat_count, dtype=jnp.int32)
    earlier = (flat_ids[:, None] > flat_ids[None, :]).astype(jnp.float32)
    before = jnp.dot(earlier, onehot, precision=lax.Precision.HIGHEST)
    return jnp.sum(before * onehot, axis=1).astype(jnp.int32).reshape(tok_rows, top_count)


def per_device(
    queries,
    new_keys,
    new_values,
    long_keys,
    long_values,
    long_lengths,
    short_keys,
    short_values,
    short_lengths,
    parents,
    accepted,
    residual,
    out_weight,
    norm_gain,
    routes,
    route_weights,
    expert_gate,
    expert_up,
    expert_down,
):
    reached = ancestors(parents)
    slot_index = slot_of(routes)
    tok_rows, top_count = routes.shape
    devices = lax.axis_size("req") * lax.axis_size("exp")
    pieces = max(1, devices // EXPERTS)
    capacity = 2 * tok_rows * top_count // EXPERTS
    target = routes * capacity + slot_index
    columns = jnp.arange(EXPERTS * pieces * capacity, dtype=jnp.int32)
    column_target = (columns // (pieces * capacity)) * capacity + columns % capacity
    hits = target[:, :, None] == column_target[None, None, :]
    placement = jnp.any(hits, axis=1).astype(jnp.bfloat16)
    weighing = jnp.sum(jnp.where(hits, route_weights[:, :, None], 0.0), axis=1)
    terms = []
    for _ in range(3):
        term = weighing.astype(jnp.bfloat16)
        terms.append(term)
        weighing = weighing - term.astype(jnp.float32)
    terms = jnp.concatenate(terms, axis=0)
    reached, placement, terms = lax.optimization_barrier((reached, placement, terms))
    head_width = new_keys.shape[2]
    stacked = jnp.concatenate([new_keys, new_values], axis=2)
    compacted = compact_path(reached, accepted, stacked)
    accepted_keys = compacted[:, :, :head_width]
    accepted_values = compacted[:, :, head_width:]
    long_out = attend(
        queries[:1], long_keys, long_values, long_lengths, new_keys[:1], new_values[:1], reached[:1]
    )
    short_out = attend(
        queries[1:],
        short_keys,
        short_values,
        short_lengths,
        new_keys[1:],
        new_values[1:],
        reached[1:],
    )
    attended = jnp.concatenate([long_out, short_out], axis=0).reshape(-1, head_width)
    n_exp = lax.axis_size("exp")
    model_width = out_weight.shape[1]
    attn_proj = ring_reduce_scatter(attended, out_weight, n_exp)
    middle = residual + attn_proj
    normed = (
        middle * lax.rsqrt(jnp.mean(middle * middle, axis=1, keepdims=True) + 1e-05) * norm_gain
    ).astype(jnp.bfloat16)
    packed = jnp.einsum("tc,td->cd", placement, normed, preferred_element_type=jnp.float32).astype(
        jnp.bfloat16
    )
    outgoing = packed.reshape(devices, capacity, model_width)
    received = lax.all_to_all(outgoing, ("req", "exp"), split_axis=0, concat_axis=0, tiled=True)
    produced = expert_rows(
        received.reshape(-1, model_width), expert_gate[0], expert_up[0], expert_down[0]
    ).reshape(devices, capacity, model_width)
    returned = lax.all_to_all(produced, ("req", "exp"), split_axis=0, concat_axis=0, tiled=True)
    moe = jnp.dot(terms, returned.reshape(-1, model_width), preferred_element_type=jnp.float32)
    moe = jnp.sum(moe.reshape(3, tok_rows, model_width), axis=0)
    hidden_out = (middle + moe).astype(jnp.bfloat16)
    return (hidden_out, accepted_keys, accepted_values)


def solution(mesh):
    in_specs = (
        P("req", None, "exp"),
        P("req", None, "exp"),
        P("req", None, "exp"),
        P("req", None, "exp"),
        P("req", None, "exp"),
        P("req"),
        P("req", None, "exp"),
        P("req", None, "exp"),
        P("req"),
        P("req", None),
        P("req"),
        P(("req", "exp"), None),
        P("exp", None),
        P(),
        P(("req", "exp"), None),
        P(("req", "exp"), None),
        P(("req", "exp"), None, None),
        P(("req", "exp"), None, None),
        P(("req", "exp"), None, None),
    )
    out_specs = (P(("req", "exp"), None), P("req", None, "exp"), P("req", None, "exp"))
    return jax.shard_map(
        per_device, mesh=mesh, in_specs=in_specs, out_specs=out_specs, check_vma=False
    )
```

```python
import jax
import jax.numpy as jnp
from jax import lax
from jax.sharding import PartitionSpec as P

HEAD = 128
EXPERTS = 64


def ancestors(parents):
    tokens_per = parents.shape[1]
    position = jnp.arange(tokens_per, dtype=jnp.int32)
    identity = (position[:, None] == position[None, :]).astype(jnp.float32)
    linked = (parents[:, :, None] == position[None, None, :]) & (position[None, :, None] > 0)
    reached = jnp.maximum(identity[None], linked.astype(jnp.float32))
    for rounds in range(tokens_per.bit_length()):
        squared = reached.astype(jnp.bfloat16)
        reached = jnp.minimum(
            jnp.einsum("bij,bjk->bik", squared, squared, preferred_element_type=jnp.float32), 1.0
        )
    return reached


def compact_path(reached, accepted, stacked):
    tokens_per = reached.shape[1]
    position = jnp.arange(tokens_per, dtype=jnp.int32)
    levels = jnp.sum(reached, axis=2) - 1.0
    leaf_row = (accepted[:, None] == position[None, :]).astype(jnp.float32)
    on_path = jnp.einsum(
        "bi,bij->bj",
        leaf_row.astype(jnp.bfloat16),
        reached.astype(jnp.bfloat16),
        preferred_element_type=jnp.float32,
    )
    chooser = on_path[:, None, :] * (
        levels[:, None, :] == position[None, :, None].astype(jnp.float32)
    ).astype(jnp.float32)
    return jnp.einsum(
        "btj,bjc->btc", chooser.astype(jnp.bfloat16), stacked, preferred_element_type=jnp.float32
    ).astype(jnp.bfloat16)


def attend(queries, cache_keys, cache_values, lengths, new_keys, new_values, reached):
    batch, tokens_per, width = queries.shape
    heads = width // HEAD
    scale = HEAD ** (-0.5)
    shape_q = (batch, tokens_per, heads, HEAD)
    shape_c = (batch, cache_keys.shape[1], heads, HEAD)
    query_four = queries.reshape(shape_q)
    cache_scores = (
        jnp.einsum(
            "bthe,blhe->bhtl",
            query_four,
            cache_keys.reshape(shape_c),
            preferred_element_type=jnp.float32,
        )
        * scale
    )
    valid = jnp.arange(cache_keys.shape[1], dtype=jnp.int32)[None, :] < lengths[:, None]
    cache_scores = jnp.where(valid[:, None, None, :], cache_scores, -jnp.inf)
    draft_scores = (
        jnp.einsum(
            "bthe,bshe->bhts",
            query_four,
            new_keys.reshape(shape_q),
            preferred_element_type=jnp.float32,
        )
        * scale
    )
    draft_scores = jnp.where(reached[:, None] > 0.5, draft_scores, -jnp.inf)
    highest = jnp.maximum(jnp.max(cache_scores, axis=3), jnp.max(draft_scores, axis=3))
    cache_probs = jnp.exp(cache_scores - highest[..., None])
    draft_probs = jnp.exp(draft_scores - highest[..., None])
    totals = jnp.sum(cache_probs, axis=3) + jnp.sum(draft_probs, axis=3)
    mixed = jnp.einsum(
        "bhtl,blhe->bthe",
        cache_probs.astype(jnp.bfloat16),
        cache_values.reshape(shape_c),
        preferred_element_type=jnp.float32,
    )
    mixed = mixed + jnp.einsum(
        "bhts,bshe->bthe",
        draft_probs.astype(jnp.bfloat16),
        new_values.reshape(shape_q),
        preferred_element_type=jnp.float32,
    )
    mixed = mixed / jnp.transpose(totals, (0, 2, 1))[..., None]
    return mixed.reshape(batch, tokens_per, width).astype(jnp.bfloat16)


def expert_rows(rows, expert_gate, expert_up, expert_down):
    gate_part = jnp.dot(rows, expert_gate, preferred_element_type=jnp.float32)
    up_part = jnp.dot(rows, expert_up, preferred_element_type=jnp.float32)
    activation = (jax.nn.silu(gate_part) * up_part).astype(jnp.bfloat16)
    return jnp.dot(activation, expert_down, preferred_element_type=jnp.float32).astype(jnp.bfloat16)


def ring_sum(blocks, shifts):
    total = blocks[0].astype(jnp.float32)
    for step, pairs in enumerate(shifts, start=1):
        total = total + lax.ppermute(blocks[step], "exp", pairs).astype(jnp.float32)
    return total


def ring_reduce_scatter(attended, out_weight, n_exp):
    side = 4
    assert n_exp == side * side
    index = lax.axis_index("exp")
    z_pos, x_pos = index // side, index % side
    cells = [(z, x) for z in range(side) for x in range(side)]
    x_shifts = [[(z * side + x, z * side + (x + k) % side) for z, x in cells] for k in range(1, side)]
    z_shifts = [[(z * side + x, ((z + k) % side) * side + x) for z, x in cells] for k in range(1, side)]
    rows = attended.shape[0] // n_exp
    width = out_weight.shape[1]
    split = width // 2
    blocks = attended.reshape(n_exp, rows, -1)
    near = jnp.arange(side, dtype=jnp.int32)
    z_of = (z_pos + near) % side
    x_of = (x_pos + near) % side
    x_major = (x_of[:, None] + z_of[None, :] * side).reshape(-1)
    z_major = (z_of[:, None] * side + x_of[None, :]).reshape(-1)
    def offset_blocks(order, weight):
        parts = []
        for step in range(side):
            picked = jnp.take(blocks, order[step * side:(step + 1) * side], axis=0)
            part = jnp.dot(picked.reshape(side * rows, -1), weight, preferred_element_type=jnp.float32)
            parts.append(part.astype(jnp.bfloat16))
        return parts

    first = offset_blocks(x_major, out_weight[:, :split])
    second = offset_blocks(z_major, out_weight[:, split:])
    first, second = lax.optimization_barrier((first, second))
    first = ring_sum(first, x_shifts)
    second = ring_sum(second, z_shifts)
    first = ring_sum(first.astype(jnp.bfloat16).reshape(side, rows, split), z_shifts)
    second = ring_sum(second.astype(jnp.bfloat16).reshape(side, rows, split), x_shifts)
    return jnp.concatenate([first, second], axis=1)


def per_device(
    queries,
    new_keys,
    new_values,
    long_keys,
    long_values,
    long_lengths,
    short_keys,
    short_values,
    short_lengths,
    parents,
    accepted,
    residual,
    out_weight,
    norm_gain,
    routes,
    route_weights,
    expert_gate,
    expert_up,
    expert_down,
):
    reached = ancestors(parents)
    head_width = new_keys.shape[2]
    stacked = jnp.concatenate([new_keys, new_values], axis=2)
    compacted = compact_path(reached, accepted, stacked)
    accepted_keys = compacted[:, :, :head_width]
    accepted_values = compacted[:, :, head_width:]
    long_out = attend(
        queries[:1], long_keys, long_values, long_lengths, new_keys[:1], new_values[:1], reached[:1]
    )
    short_out = attend(
        queries[1:],
        short_keys,
        short_values,
        short_lengths,
        new_keys[1:],
        new_values[1:],
        reached[1:],
    )
    attended = jnp.concatenate([long_out, short_out], axis=0).reshape(-1, head_width)
    n_exp = lax.axis_size("exp")
    model_width = out_weight.shape[1]
    attn_proj = ring_reduce_scatter(attended, out_weight, n_exp)
    middle = residual + attn_proj
    normed = (
        middle * lax.rsqrt(jnp.mean(middle * middle, axis=1, keepdims=True) + 1e-05) * norm_gain
    ).astype(jnp.bfloat16)
    tok_rows, top_count = routes.shape
    devices = lax.axis_size("req") * lax.axis_size("exp")
    pieces = max(1, devices // EXPERTS)
    capacity = 2 * tok_rows * top_count // EXPERTS
    flat_routes = routes.reshape(-1)
    flat_count = flat_routes.shape[0]
    expert_ids = jnp.arange(EXPERTS, dtype=jnp.int32)
    onehot = (flat_routes[:, None] == expert_ids[None, :]).astype(jnp.float32)
    flat_ids = jnp.arange(flat_count, dtype=jnp.int32)
    earlier = (flat_ids[:, None] > flat_ids[None, :]).astype(jnp.float32)
    before = jnp.dot(earlier, onehot, precision=lax.Precision.HIGHEST)
    slot_index = jnp.sum(before * onehot, axis=1).astype(jnp.int32).reshape(tok_rows, top_count)
    target = routes * capacity + slot_index
    columns = jnp.arange(EXPERTS * pieces * capacity, dtype=jnp.int32)
    column_target = (columns // (pieces * capacity)) * capacity + columns % capacity
    hits = target[:, :, None] == column_target[None, None, :]
    placement = jnp.any(hits, axis=1).astype(jnp.bfloat16)
    packed = jnp.einsum("tc,td->cd", placement, normed, preferred_element_type=jnp.float32).astype(
        jnp.bfloat16
    )
    outgoing = packed.reshape(devices, capacity, model_width)
    received = lax.all_to_all(outgoing, ("req", "exp"), split_axis=0, concat_axis=0, tiled=True)
    produced = expert_rows(
        received.reshape(-1, model_width), expert_gate[0], expert_up[0], expert_down[0]
    ).reshape(devices, capacity, model_width)
    returned = lax.all_to_all(produced, ("req", "exp"), split_axis=0, concat_axis=0, tiled=True)
    weighing = jnp.sum(jnp.where(hits, route_weights[:, :, None], 0.0), axis=1)
    terms = []
    for _ in range(3):
        term = weighing.astype(jnp.bfloat16)
        terms.append(term)
        weighing = weighing - term.astype(jnp.float32)
    terms = jnp.concatenate(terms, axis=0)
    moe = jnp.dot(terms, returned.reshape(-1, model_width), preferred_element_type=jnp.float32)
    moe = jnp.sum(moe.reshape(3, tok_rows, model_width), axis=0)
    hidden_out = (middle + moe).astype(jnp.bfloat16)
    return (hidden_out, accepted_keys, accepted_values)


def solution(mesh):
    in_specs = (
        P("req", None, "exp"),
        P("req", None, "exp"),
        P("req", None, "exp"),
        P("req", None, "exp"),
        P("req", None, "exp"),
        P("req"),
        P("req", None, "exp"),
        P("req", None, "exp"),
        P("req"),
        P("req", None),
        P("req"),
        P(("req", "exp"), None),
        P("exp", None),
        P(),
        P(("req", "exp"), None),
        P(("req", "exp"), None),
        P(("req", "exp"), None, None),
        P(("req", "exp"), None, None),
        P(("req", "exp"), None, None),
    )
    out_specs = (P(("req", "exp"), None), P("req", None, "exp"), P("req", None, "exp"))
    return jax.shard_map(
        per_device, mesh=mesh, in_specs=in_specs, out_specs=out_specs, check_vma=False
    )
```

```python
import jax
import jax.numpy as jnp
from jax import lax
from jax.sharding import PartitionSpec as P

HEAD = 128
EXPERTS = 64


def ancestors(parents):
    tokens_per = parents.shape[1]
    position = jnp.arange(tokens_per, dtype=jnp.int32)
    identity = (position[:, None] == position[None, :]).astype(jnp.float32)
    linked = (parents[:, :, None] == position[None, None, :]) & (position[None, :, None] > 0)
    reached = jnp.maximum(identity[None], linked.astype(jnp.float32))
    for rounds in range(tokens_per.bit_length()):
        squared = reached.astype(jnp.bfloat16)
        reached = jnp.minimum(
            jnp.einsum("bij,bjk->bik", squared, squared, preferred_element_type=jnp.float32), 1.0
        )
    return reached


def compact_path(reached, accepted, stacked):
    tokens_per = reached.shape[1]
    position = jnp.arange(tokens_per, dtype=jnp.int32)
    levels = jnp.sum(reached, axis=2) - 1.0
    leaf_row = (accepted[:, None] == position[None, :]).astype(jnp.float32)
    on_path = jnp.einsum(
        "bi,bij->bj",
        leaf_row.astype(jnp.bfloat16),
        reached.astype(jnp.bfloat16),
        preferred_element_type=jnp.float32,
    )
    chooser = on_path[:, None, :] * (
        levels[:, None, :] == position[None, :, None].astype(jnp.float32)
    ).astype(jnp.float32)
    return jnp.einsum(
        "btj,bjc->btc", chooser.astype(jnp.bfloat16), stacked, preferred_element_type=jnp.float32
    ).astype(jnp.bfloat16)


def attend(queries, cache_keys, cache_values, lengths, new_keys, new_values, reached):
    batch, tokens_per, width = queries.shape
    heads = width // HEAD
    scale = HEAD ** (-0.5)
    shape_q = (batch, tokens_per, heads, HEAD)
    shape_c = (batch, cache_keys.shape[1], heads, HEAD)
    query_four = queries.reshape(shape_q)
    cache_scores = (
        jnp.einsum(
            "bthe,blhe->bhtl",
            query_four,
            cache_keys.reshape(shape_c),
            preferred_element_type=jnp.float32,
        )
        * scale
    )
    valid = jnp.arange(cache_keys.shape[1], dtype=jnp.int32)[None, :] < lengths[:, None]
    cache_scores = jnp.where(valid[:, None, None, :], cache_scores, -jnp.inf)
    draft_scores = (
        jnp.einsum(
            "bthe,bshe->bhts",
            query_four,
            new_keys.reshape(shape_q),
            preferred_element_type=jnp.float32,
        )
        * scale
    )
    draft_scores = jnp.where(reached[:, None] > 0.5, draft_scores, -jnp.inf)
    highest = jnp.maximum(jnp.max(cache_scores, axis=3), jnp.max(draft_scores, axis=3))
    cache_probs = jnp.exp(cache_scores - highest[..., None])
    draft_probs = jnp.exp(draft_scores - highest[..., None])
    totals = jnp.sum(cache_probs, axis=3) + jnp.sum(draft_probs, axis=3)
    mixed = jnp.einsum(
        "bhtl,blhe->bthe",
        cache_probs.astype(jnp.bfloat16),
        cache_values.reshape(shape_c),
        preferred_element_type=jnp.float32,
    )
    mixed = mixed + jnp.einsum(
        "bhts,bshe->bthe",
        draft_probs.astype(jnp.bfloat16),
        new_values.reshape(shape_q),
        preferred_element_type=jnp.float32,
    )
    mixed = mixed / jnp.transpose(totals, (0, 2, 1))[..., None]
    return mixed.reshape(batch, tokens_per, width).astype(jnp.bfloat16)


def expert_rows(rows, expert_gate, expert_up, expert_down):
    both = jnp.dot(
        rows, jnp.concatenate([expert_gate, expert_up], axis=1), preferred_element_type=jnp.float32
    )
    gate_part, up_part = jnp.split(both, 2, axis=1)
    activation = (jax.nn.silu(gate_part) * up_part).astype(jnp.bfloat16)
    return jnp.dot(activation, expert_down, preferred_element_type=jnp.float32).astype(jnp.bfloat16)


def ring_sum(blocks, shifts):
    total = blocks[0].astype(jnp.float32)
    for step, pairs in enumerate(shifts, start=1):
        total = total + lax.ppermute(blocks[step], "exp", pairs).astype(jnp.float32)
    return total


def ring_reduce_scatter(attended, out_weight, n_exp):
    side = 4
    assert n_exp == side * side
    index = lax.axis_index("exp")
    z_pos, x_pos = index // side, index % side
    cells = [(z, x) for z in range(side) for x in range(side)]
    x_shifts = [[(z * side + x, z * side + (x + k) % side) for z, x in cells] for k in range(1, side)]
    z_shifts = [[(z * side + x, ((z + k) % side) * side + x) for z, x in cells] for k in range(1, side)]
    rows = attended.shape[0] // n_exp
    width = out_weight.shape[1]
    split = width // 2
    blocks = attended.reshape(n_exp, rows, -1)
    near = jnp.arange(side, dtype=jnp.int32)
    z_of = (z_pos + near) % side
    x_of = (x_pos + near) % side
    x_major = (x_of[:, None] + z_of[None, :] * side).reshape(-1)
    z_major = (z_of[:, None] * side + x_of[None, :]).reshape(-1)
    first = jnp.take(blocks, x_major, axis=0).reshape(n_exp * rows, -1)
    first = jnp.dot(first, out_weight[:, :split], preferred_element_type=jnp.float32)
    first = first.astype(jnp.bfloat16).reshape(side, side * rows, split)
    second = jnp.take(blocks, z_major, axis=0).reshape(n_exp * rows, -1)
    second = jnp.dot(second, out_weight[:, split:], preferred_element_type=jnp.float32)
    second = second.astype(jnp.bfloat16).reshape(side, side * rows, split)
    first, second = lax.optimization_barrier((first, second))
    first = ring_sum(first, x_shifts)
    second = ring_sum(second, z_shifts)
    first = ring_sum(first.astype(jnp.bfloat16).reshape(side, rows, split), z_shifts)
    second = ring_sum(second.astype(jnp.bfloat16).reshape(side, rows, split), x_shifts)
    return jnp.concatenate([first, second], axis=1)


def per_device(
    queries,
    new_keys,
    new_values,
    long_keys,
    long_values,
    long_lengths,
    short_keys,
    short_values,
    short_lengths,
    parents,
    accepted,
    residual,
    out_weight,
    norm_gain,
    routes,
    route_weights,
    expert_gate,
    expert_up,
    expert_down,
):
    reached = ancestors(parents)
    head_width = new_keys.shape[2]
    stacked = jnp.concatenate([new_keys, new_values], axis=2)
    compacted = compact_path(reached, accepted, stacked)
    accepted_keys = compacted[:, :, :head_width]
    accepted_values = compacted[:, :, head_width:]
    long_out = attend(
        queries[:1], long_keys, long_values, long_lengths, new_keys[:1], new_values[:1], reached[:1]
    )
    short_out = attend(
        queries[1:],
        short_keys,
        short_values,
        short_lengths,
        new_keys[1:],
        new_values[1:],
        reached[1:],
    )
    attended = jnp.concatenate([long_out, short_out], axis=0).reshape(-1, head_width)
    n_exp = lax.axis_size("exp")
    model_width = out_weight.shape[1]
    attn_proj = ring_reduce_scatter(attended, out_weight, n_exp)
    middle = residual + attn_proj
    normed = (
        middle * lax.rsqrt(jnp.mean(middle * middle, axis=1, keepdims=True) + 1e-05) * norm_gain
    ).astype(jnp.bfloat16)
    tok_rows, top_count = routes.shape
    devices = lax.axis_size("req") * lax.axis_size("exp")
    pieces = max(1, devices // EXPERTS)
    capacity = 2 * tok_rows * top_count // EXPERTS
    flat_routes = routes.reshape(-1)
    flat_count = flat_routes.shape[0]
    expert_ids = jnp.arange(EXPERTS, dtype=jnp.int32)
    onehot = (flat_routes[:, None] == expert_ids[None, :]).astype(jnp.float32)
    flat_ids = jnp.arange(flat_count, dtype=jnp.int32)
    earlier = (flat_ids[:, None] > flat_ids[None, :]).astype(jnp.float32)
    before = jnp.dot(earlier, onehot, precision=lax.Precision.HIGHEST)
    slot_index = jnp.sum(before * onehot, axis=1).astype(jnp.int32).reshape(tok_rows, top_count)
    target = routes * capacity + slot_index
    columns = jnp.arange(EXPERTS * pieces * capacity, dtype=jnp.int32)
    column_target = (columns // (pieces * capacity)) * capacity + columns % capacity
    hits = target[:, :, None] == column_target[None, None, :]
    placement = jnp.any(hits, axis=1).astype(jnp.bfloat16)
    packed = jnp.einsum("tc,td->cd", placement, normed, preferred_element_type=jnp.float32).astype(
        jnp.bfloat16
    )
    outgoing = packed.reshape(devices, capacity, model_width)
    received = lax.all_to_all(outgoing, ("req", "exp"), split_axis=0, concat_axis=0, tiled=True)
    produced = expert_rows(
        received.reshape(-1, model_width), expert_gate[0], expert_up[0], expert_down[0]
    ).reshape(devices, capacity, model_width)
    returned = lax.all_to_all(produced, ("req", "exp"), split_axis=0, concat_axis=0, tiled=True)
    weighing = jnp.sum(jnp.where(hits, route_weights[:, :, None], 0.0), axis=1)
    terms = []
    for _ in range(3):
        term = weighing.astype(jnp.bfloat16)
        terms.append(term)
        weighing = weighing - term.astype(jnp.float32)
    terms = jnp.concatenate(terms, axis=0)
    moe = jnp.dot(terms, returned.reshape(-1, model_width), preferred_element_type=jnp.float32)
    moe = jnp.sum(moe.reshape(3, tok_rows, model_width), axis=0)
    hidden_out = (middle + moe).astype(jnp.bfloat16)
    return (hidden_out, accepted_keys, accepted_values)


def solution(mesh):
    in_specs = (
        P("req", None, "exp"),
        P("req", None, "exp"),
        P("req", None, "exp"),
        P("req", None, "exp"),
        P("req", None, "exp"),
        P("req"),
        P("req", None, "exp"),
        P("req", None, "exp"),
        P("req"),
        P("req", None),
        P("req"),
        P(("req", "exp"), None),
        P("exp", None),
        P(),
        P(("req", "exp"), None),
        P(("req", "exp"), None),
        P(("req", "exp"), None, None),
        P(("req", "exp"), None, None),
        P(("req", "exp"), None, None),
    )
    out_specs = (P(("req", "exp"), None), P("req", None, "exp"), P("req", None, "exp"))
    return jax.shard_map(
        per_device, mesh=mesh, in_specs=in_specs, out_specs=out_specs, check_vma=False
    )
```

```python
import jax
import jax.numpy as jnp
from jax import lax
from jax.sharding import PartitionSpec as P

HEAD = 128
EXPERTS = 64


def ancestors(parents):
    tokens_per = parents.shape[1]
    position = jnp.arange(tokens_per, dtype=jnp.int32)
    identity = (position[:, None] == position[None, :]).astype(jnp.float32)
    linked = (parents[:, :, None] == position[None, None, :]) & (position[None, :, None] > 0)
    reached = jnp.maximum(identity[None], linked.astype(jnp.float32))
    for rounds in range(tokens_per.bit_length()):
        squared = reached.astype(jnp.bfloat16)
        reached = jnp.minimum(
            jnp.einsum("bij,bjk->bik", squared, squared, preferred_element_type=jnp.float32), 1.0
        )
    return reached


def compact_path(reached, accepted, stacked):
    tokens_per = reached.shape[1]
    position = jnp.arange(tokens_per, dtype=jnp.int32)
    levels = jnp.sum(reached, axis=2) - 1.0
    leaf_row = (accepted[:, None] == position[None, :]).astype(jnp.float32)
    on_path = jnp.einsum(
        "bi,bij->bj",
        leaf_row.astype(jnp.bfloat16),
        reached.astype(jnp.bfloat16),
        preferred_element_type=jnp.float32,
    )
    chooser = on_path[:, None, :] * (
        levels[:, None, :] == position[None, :, None].astype(jnp.float32)
    ).astype(jnp.float32)
    return jnp.einsum(
        "btj,bjc->btc", chooser.astype(jnp.bfloat16), stacked, preferred_element_type=jnp.float32
    ).astype(jnp.bfloat16)


def attend(queries, cache_keys, cache_values, lengths, new_keys, new_values, reached):
    batch, tokens_per, width = queries.shape
    heads = width // HEAD
    scale = HEAD ** (-0.5)
    shape_q = (batch, tokens_per, heads, HEAD)
    shape_c = (batch, cache_keys.shape[1], heads, HEAD)
    query_four = queries.reshape(shape_q)
    cache_scores = (
        jnp.einsum(
            "bthe,blhe->bhtl",
            query_four,
            cache_keys.reshape(shape_c),
            preferred_element_type=jnp.float32,
        )
        * scale
    )
    valid = jnp.arange(cache_keys.shape[1], dtype=jnp.int32)[None, :] < lengths[:, None]
    cache_scores = jnp.where(valid[:, None, None, :], cache_scores, -jnp.inf)
    draft_scores = (
        jnp.einsum(
            "bthe,bshe->bhts",
            query_four,
            new_keys.reshape(shape_q),
            preferred_element_type=jnp.float32,
        )
        * scale
    )
    draft_scores = jnp.where(reached[:, None] > 0.5, draft_scores, -jnp.inf)
    highest = jnp.maximum(jnp.max(cache_scores, axis=3), jnp.max(draft_scores, axis=3))
    cache_probs = jnp.exp(cache_scores - highest[..., None])
    draft_probs = jnp.exp(draft_scores - highest[..., None])
    totals = jnp.sum(cache_probs, axis=3) + jnp.sum(draft_probs, axis=3)
    mixed = jnp.einsum(
        "bhtl,blhe->bthe",
        cache_probs.astype(jnp.bfloat16),
        cache_values.reshape(shape_c),
        preferred_element_type=jnp.float32,
    )
    mixed = mixed + jnp.einsum(
        "bhts,bshe->bthe",
        draft_probs.astype(jnp.bfloat16),
        new_values.reshape(shape_q),
        preferred_element_type=jnp.float32,
    )
    mixed = mixed / jnp.transpose(totals, (0, 2, 1))[..., None]
    return mixed.reshape(batch, tokens_per, width).astype(jnp.bfloat16)


def expert_rows(rows, expert_gate, expert_up, expert_down):
    gate_part = jnp.dot(rows, expert_gate, preferred_element_type=jnp.float32)
    up_part = jnp.dot(rows, expert_up, preferred_element_type=jnp.float32)
    activation = (jax.nn.silu(gate_part) * up_part).astype(jnp.bfloat16)
    return jnp.dot(activation, expert_down, preferred_element_type=jnp.float32).astype(jnp.bfloat16)


def ring_sum(blocks, shifts):
    total = blocks[0].astype(jnp.float32)
    for step, pairs in enumerate(shifts, start=1):
        total = total + lax.ppermute(blocks[step], "exp", pairs).astype(jnp.float32)
    return total


def ring_reduce_scatter(attended, out_weight, n_exp):
    side = 4
    assert n_exp == side * side
    index = lax.axis_index("exp")
    z_pos, x_pos = index // side, index % side
    cells = [(z, x) for z in range(side) for x in range(side)]
    x_shifts = [[(z * side + x, z * side + (x + k) % side) for z, x in cells] for k in range(1, side)]
    z_shifts = [[(z * side + x, ((z + k) % side) * side + x) for z, x in cells] for k in range(1, side)]
    rows = attended.shape[0] // n_exp
    width = out_weight.shape[1]
    split = width // 2
    blocks = attended.reshape(n_exp, rows, -1)
    near = jnp.arange(side, dtype=jnp.int32)
    z_of = (z_pos + near) % side
    x_of = (x_pos + near) % side
    x_major = (x_of[:, None] + z_of[None, :] * side).reshape(-1)
    z_major = (z_of[:, None] * side + x_of[None, :]).reshape(-1)
    first = jnp.take(blocks, x_major, axis=0).reshape(n_exp * rows, -1)
    first = jnp.dot(first, out_weight[:, :split], preferred_element_type=jnp.float32)
    first = first.astype(jnp.bfloat16).reshape(side, side * rows, split)
    second = jnp.take(blocks, z_major, axis=0).reshape(n_exp * rows, -1)
    second = jnp.dot(second, out_weight[:, split:], preferred_element_type=jnp.float32)
    second = second.astype(jnp.bfloat16).reshape(side, side * rows, split)
    first, second = lax.optimization_barrier((first, second))
    first = ring_sum(first, x_shifts)
    second = ring_sum(second, z_shifts)
    first = ring_sum(first.astype(jnp.bfloat16).reshape(side, rows, split), z_shifts)
    second = ring_sum(second.astype(jnp.bfloat16).reshape(side, rows, split), x_shifts)
    return jnp.concatenate([first, second], axis=1)


def per_device(
    queries,
    new_keys,
    new_values,
    long_keys,
    long_values,
    long_lengths,
    short_keys,
    short_values,
    short_lengths,
    parents,
    accepted,
    residual,
    out_weight,
    norm_gain,
    routes,
    route_weights,
    expert_gate,
    expert_up,
    expert_down,
):
    reached = ancestors(parents)
    head_width = new_keys.shape[2]
    stacked = jnp.concatenate([new_keys, new_values], axis=2)
    compacted = compact_path(reached, accepted, stacked)
    accepted_keys = compacted[:, :, :head_width]
    accepted_values = compacted[:, :, head_width:]
    long_out = attend(
        queries[:1], long_keys, long_values, long_lengths, new_keys[:1], new_values[:1], reached[:1]
    )
    short_out = attend(
        queries[1:],
        short_keys,
        short_values,
        short_lengths,
        new_keys[1:],
        new_values[1:],
        reached[1:],
    )
    attended = jnp.concatenate([long_out, short_out], axis=0).reshape(-1, head_width)
    n_exp = lax.axis_size("exp")
    model_width = out_weight.shape[1]
    attn_proj = ring_reduce_scatter(attended, out_weight, n_exp)
    middle = residual + attn_proj
    normed = (
        middle * lax.rsqrt(jnp.mean(middle * middle, axis=1, keepdims=True) + 1e-05) * norm_gain
    ).astype(jnp.bfloat16)
    tok_rows, top_count = routes.shape
    devices = lax.axis_size("req") * lax.axis_size("exp")
    pieces = max(1, devices // EXPERTS)
    capacity = 2 * tok_rows * top_count // EXPERTS
    flat_routes = routes.reshape(-1)
    flat_count = flat_routes.shape[0]
    expert_ids = jnp.arange(EXPERTS, dtype=jnp.int32)
    onehot = (flat_routes[:, None] == expert_ids[None, :]).astype(jnp.float32)
    flat_ids = jnp.arange(flat_count, dtype=jnp.int32)
    earlier = (flat_ids[:, None] > flat_ids[None, :]).astype(jnp.float32)
    before = jnp.dot(earlier, onehot, precision=lax.Precision.HIGHEST)
    slot_index = jnp.sum(before * onehot, axis=1).astype(jnp.int32).reshape(tok_rows, top_count)
    target = routes * capacity + slot_index
    columns = jnp.arange(EXPERTS * pieces * capacity, dtype=jnp.int32)
    column_target = (columns // (pieces * capacity)) * capacity + columns % capacity
    hits = target[:, :, None] == column_target[None, None, :]
    placement = jnp.any(hits, axis=1).astype(jnp.bfloat16)
    packed = jnp.einsum("tc,td->cd", placement, normed, preferred_element_type=jnp.float32).astype(
        jnp.bfloat16
    )
    outgoing = packed.reshape(devices, capacity, model_width)
    received = lax.all_to_all(outgoing, ("req", "exp"), split_axis=0, concat_axis=0, tiled=True)
    produced = expert_rows(
        received.reshape(-1, model_width), expert_gate[0], expert_up[0], expert_down[0]
    ).reshape(devices, capacity, model_width)
    returned = lax.all_to_all(produced, ("req", "exp"), split_axis=0, concat_axis=0, tiled=True)
    weighing = jnp.sum(jnp.where(hits, route_weights[:, :, None], 0.0), axis=1)
    terms = []
    for _ in range(2):
        term = weighing.astype(jnp.bfloat16)
        terms.append(term)
        weighing = weighing - term.astype(jnp.float32)
    terms = jnp.concatenate(terms, axis=0)
    moe = jnp.dot(terms, returned.reshape(-1, model_width), preferred_element_type=jnp.float32)
    moe = jnp.sum(moe.reshape(2, tok_rows, model_width), axis=0)
    hidden_out = (middle + moe).astype(jnp.bfloat16)
    return (hidden_out, accepted_keys, accepted_values)


def solution(mesh):
    in_specs = (
        P("req", None, "exp"),
        P("req", None, "exp"),
        P("req", None, "exp"),
        P("req", None, "exp"),
        P("req", None, "exp"),
        P("req"),
        P("req", None, "exp"),
        P("req", None, "exp"),
        P("req"),
        P("req", None),
        P("req"),
        P(("req", "exp"), None),
        P("exp", None),
        P(),
        P(("req", "exp"), None),
        P(("req", "exp"), None),
        P(("req", "exp"), None, None),
        P(("req", "exp"), None, None),
        P(("req", "exp"), None, None),
    )
    out_specs = (P(("req", "exp"), None), P("req", None, "exp"), P("req", None, "exp"))
    return jax.shard_map(
        per_device, mesh=mesh, in_specs=in_specs, out_specs=out_specs, check_vma=False
    )
```
